128 devices in a mesh: region: 64 (over y, x, z), rep: 2 (over core).
Axes of the slice: x: 4, y: 4, z: 4, core: 2. Of those that a mesh axis runs over, the one named last changes fastest.
Arguments:
- emb: bfloat16 [262144, 128], P('region'), may hold values from -6 to 6
- lengths: bfloat16 [6144, 14, 128, 128], P(('region', 'rep')), may hold values from 0 to 0.003616333
- pair_block: int32 [6144, 14], P(('region', 'rep')), may hold values from 0 to 255, as said below
- feats: bfloat16 [16, 786432], P(None, ('region', 'rep')), may hold values from -6 to 6
- proj: bfloat16 [16, 128], replicated, may hold values from -1.5 to 1.5
- targets: float32 [786432], P(('region', 'rep')), may hold values from -6 to 6
- trip_weight: float32 [786432], P(('region', 'rep')), may hold values from 0.5 to 5
- send_list: int32 [64, 2, 64, 4], P('region', 'rep'), may hold values from -1 to 31, as said below
- nb_index: int32 [64, 4, 4096], P('region'), may hold values from 0 to 4351, as said below
- nb_weight: float32 [64, 4, 4096], P('region'), may hold values from 0.2 to 1
Outputs:
- predicted: float32 [786432], P(('region', 'rep'))
- gradient: bfloat16 [262144, 128], P('region')
The draws below stay inside these ranges and needn't reach their ends.
Inputs may be any that keep to these rules, and one draw needn't show every extreme that they name: `send_list`: entry [q, p, r, j] names a block of region q's embedding rows that region r's device with rep index p needs; in each list over j the live entries come first and the rest are -1; each list holds 1 to 4 live entries and some hold exactly 4. `pair_block`: entry [t, k] is q * 4 + j for a live slot j of the list that region q sends to the device holding trip block t. `nb_index`: entry [r, k, i] is a position in region r's rows extended by 128 rows of each neighbouring region on either side (regions wrap around); it differs from the segment's own position i + 128 by 1 to 128.
All inputs are finite; a program needn't handle non-finite values.
Results may differ from the reference program's by a relative error of at most 0.0034.
Values may be sent and summed in bfloat16 or wider, within the bound.
No kernel may reach another device: no remote copies, remote signals or barrier semaphores. Data moves between devices by JAX's collectives and lax.ppermute only.
A program may use at most 192 MiB of HBM per device.

```python
import math
import jax
import jax.numpy as jnp
from jax import lax

RANK = 128
BLOCK = 128
TFEAT = 16
SEG_BLK_DEV = 32
TB_DEV = 48
KB = 14
SLOTS = 4
NB = 4
HALO = 128
REGIONS = 64
REPS = 2
SEG_DEV = 4096
SEGS = 262144
TRIP_DEV = 6144
TB_ALL = 6144
TRIPS = 786432
DEVICES = 128


def slot_counts(key):
    base_key = jax.random.fold_in(key, 11)
    counts = jax.random.randint(jax.random.fold_in(base_key, 1), (REGIONS, REPS, REGIONS), 1, SLOTS + 1)
    hot_draw = jax.random.randint(jax.random.fold_in(base_key, 2), (REGIONS, 1, 1), 0, 4) == 0
    hot_owner = hot_draw | (jnp.arange(REGIONS)[:, None, None] == REGIONS - 1)
    return jnp.where(hot_owner, SLOTS, counts).astype(jnp.int32)


def draw_send_list(key, part):
    counts = slot_counts(key)
    picks = jax.random.randint(jax.random.fold_in(key, 21), (REGIONS, REPS, REGIONS, SLOTS), 0, SEG_BLK_DEV)
    position = jnp.arange(SLOTS)[None, None, None, :]
    return jnp.where(position < counts[..., None], picks, -1).astype(jnp.int32)


def draw_pair_block(key, part):
    counts = slot_counts(key)
    trip_block = jnp.arange(TB_ALL)
    owner_device = trip_block // TB_DEV
    region_id = (owner_device // REPS)[:, None]
    rep_id = (owner_device % REPS)[:, None]
    source = jax.random.randint(jax.random.fold_in(key, 31), (TB_ALL, KB), 0, REGIONS)
    live_count = counts[source, rep_id, region_id]
    slot_pick = jax.random.randint(jax.random.fold_in(key, 32), (TB_ALL, KB), 0, live_count)
    values = source * SLOTS + slot_pick
    corner = (trip_block[:, None] == 0) & (jnp.arange(KB)[None, :] == 0)
    return jnp.where(corner, REGIONS * SLOTS - 1, values).astype(jnp.int32)


def draw_nb_index(key, part):
    position = jnp.arange(SEG_DEV)[None, None, :]
    reach = jax.random.randint(jax.random.fold_in(key, 41), (REGIONS, NB, SEG_DEV), 1, HALO + 1)
    direction = jax.random.randint(jax.random.fold_in(key, 42), (REGIONS, NB, SEG_DEV), 0, 2) * 2 - 1
    region_ids = jnp.arange(REGIONS)[:, None, None]
    column_ids = jnp.arange(NB)[None, :, None]
    first_spot = (region_ids == 0) & (column_ids == 0) & (position == 0)
    last_spot = (region_ids == 0) & (column_ids == 0) & (position == SEG_DEV - 1)
    reach = jnp.where(first_spot | last_spot, HALO, reach)
    direction = jnp.where(first_spot, -1, jnp.where(last_spot, 1, direction))
    return (HALO + position + reach * direction).astype(jnp.int32)


def shard_levels(key, dims, pieces, least, high):
    def one(axis_at, shards_of):
        steps = jax.random.uniform(jax.random.fold_in(jax.random.fold_in(key, 6), axis_at), (shards_of,), jnp.float32, least / len(pieces), high / len(pieces))
        return jnp.repeat(jnp.exp(steps), dims[axis_at] // shards_of).reshape((-1,) + (1,) * (len(dims) - axis_at - 1))

    gain = one(*pieces[0])
    for cut in pieces[1:]:
        gain = gain * one(*cut)
    return gain


def gaussian(key, extent, deviation, bound, shards=(), kind=jnp.bfloat16):
    gain = shard_levels(key, extent, shards, -0.22, 0.18) if shards else 1.0
    entries = jax.random.normal(key, extent, jnp.float32) * deviation * gain
    return jnp.minimum(jnp.maximum(entries, -bound), bound).astype(kind)


def setup_inputs(seed: int = 0) -> dict:
    keys = jax.random.split(jax.random.key(seed), 11)
    return {
        "emb": gaussian(keys[0], (SEGS, RANK), 1.0, 6.0, ((0, 64),)),
        "lengths": jnp.clip(0.003616333 * jax.random.uniform(keys[1], (TB_ALL, KB, BLOCK, BLOCK), jnp.float32) ** shard_levels(keys[1], (TB_ALL, KB, BLOCK, BLOCK), ((0, 128),), -0.2, 0.2), 0.0, 0.003616333).astype(jnp.bfloat16),
        "pair_block": draw_pair_block(jax.random.fold_in(keys[10], 71), 0),
        "feats": gaussian(keys[3], (TFEAT, TRIPS), 1.0, 6.0, ((1, 128),)),
        "proj": gaussian(keys[4], (TFEAT, RANK), TFEAT ** -0.5, 1.5),
        "targets": gaussian(keys[5], (TRIPS,), 1.0, 6.0, ((0, 128),), jnp.float32),
        "trip_weight": jnp.clip(jnp.exp(math.log(5.0) - 2.3025851 * jax.random.uniform(keys[6], (TRIPS,), jnp.float32) ** shard_levels(keys[6], (TRIPS,), ((0, 128),), -0.2, 0.2)), 0.5, 5.0),
        "send_list": draw_send_list(jax.random.fold_in(keys[10], 71), 0),
        "nb_index": draw_nb_index(jax.random.fold_in(keys[10], 71), 0),
        "nb_weight": jnp.clip(jnp.exp(math.log(1.0) - 1.609438 * jax.random.uniform(keys[9], (REGIONS, NB, SEG_DEV), jnp.float32) ** shard_levels(keys[9], (REGIONS, NB, SEG_DEV), ((0, 64),), -0.2, 0.2)), 0.2, 1.0),
    }


LAM = 0.25


def reference(emb, lengths, pair_block, feats, proj, targets, trip_weight, send_list, nb_index, nb_weight):
    blocks = emb.reshape(REGIONS * SEG_BLK_DEV, BLOCK, RANK)
    owners = (jnp.arange(REGIONS, dtype=jnp.int32) * SEG_BLK_DEV)[:, None]

    def device_pass(accumulated, device):
        region_id = device // REPS
        rep_id = device % REPS
        send_rows = send_list[:, rep_id, region_id, :]
        live_mask = send_rows >= 0
        global_ids = jnp.where(live_mask, owners + send_rows, 0).reshape(-1).astype(jnp.int32)
        flat_live = live_mask.reshape(-1)
        first_block = (device * TB_DEV).astype(jnp.int32)
        length_rows = lax.dynamic_slice_in_dim(lengths, first_block, TB_DEV, 0)
        pair_rows = lax.dynamic_slice_in_dim(pair_block, first_block, TB_DEV, 0)
        global_pairs = global_ids[pair_rows]
        pair_mask = flat_live[pair_rows].astype(jnp.float32)
        first_trip = (device * TRIP_DEV).astype(jnp.int32)
        feat_cols = lax.dynamic_slice_in_dim(feats, first_trip, TRIP_DEV, 1)
        trip_query = jnp.dot(feat_cols.T, proj, preferred_element_type=jnp.float32)
        query_blocks = trip_query.reshape(TB_DEV, BLOCK, RANK)
        hidden_sum = jnp.zeros((TB_DEV, BLOCK, RANK), jnp.float32)
        for column in range(KB):
            picked = blocks[global_pairs[:, column]].astype(jnp.float32) * pair_mask[:, column][:, None, None]
            hidden_sum = hidden_sum + jnp.einsum('tas,tsr->tar', length_rows[:, column].astype(jnp.float32), picked)
        predicted = jnp.sum(hidden_sum * query_blocks, axis=-1).reshape(TRIP_DEV)
        target_rows = lax.dynamic_slice_in_dim(targets, first_trip, TRIP_DEV, 0)
        weight_rows = lax.dynamic_slice_in_dim(trip_weight, first_trip, TRIP_DEV, 0)
        scaled = ((weight_rows * (predicted - target_rows))[:, None] * trip_query).astype(jnp.bfloat16)
        scaled = scaled.reshape(TB_DEV, BLOCK, RANK).astype(jnp.float32)
        for column in range(KB):
            term = jnp.einsum('tas,tar->tsr', length_rows[:, column].astype(jnp.float32), scaled)
            accumulated = accumulated.at[global_pairs[:, column]].add(term * pair_mask[:, column][:, None, None])
        return accumulated, predicted

    start_grad = jnp.zeros((REGIONS * SEG_BLK_DEV, BLOCK, RANK), jnp.float32)
    data_grad, predicted = lax.scan(device_pass, start_grad, jnp.arange(DEVICES, dtype=jnp.int32))
    base_rows = (jnp.arange(REGIONS, dtype=jnp.int32) * SEG_DEV - HALO)[:, None]
    emb_float = emb.astype(jnp.float32)
    own_rows = emb_float.reshape(REGIONS, SEG_DEV, RANK)
    smooth = jnp.zeros((REGIONS, SEG_DEV, RANK), jnp.float32)
    for column in range(NB):
        neighbour_rows = ((base_rows + nb_index[:, column, :]) % SEGS).astype(jnp.int32)
        smooth = smooth + nb_weight[:, column, :, None] * (own_rows - emb_float[neighbour_rows])
    gradient = (data_grad.reshape(SEGS, RANK) + LAM * smooth.reshape(SEGS, RANK)).astype(jnp.bfloat16)
    return predicted.reshape(TRIPS), gradient
```

```python
import functools

import jax
import jax.numpy as jnp
from jax import lax
from jax.experimental import pallas as pl
from jax.experimental.pallas import tpu as pltpu
from jax.sharding import PartitionSpec as P

LAM = 0.25
F32 = jnp.float32
BF16 = jnp.bfloat16
TN = (((0,), (0,)), ((), ()))


def with_halo(cells, sides, width):
    for axis, dim in sides:
        count = lax.axis_size(axis)
        head = lax.slice_in_dim(cells, 0, width, axis=dim)
        tail = lax.slice_in_dim(cells, cells.shape[dim] - width, cells.shape[dim], axis=dim)
        cells = jnp.concatenate(
            [
                lax.ppermute(tail, axis, [(i, (i + 1) % count) for i in range(count)]),
                cells,
                lax.ppermute(head, axis, [((i + 1) % count, i) for i in range(count)]),
            ],
            axis=dim,
        )
    return cells


def trip_kernel(pair_count, pb_ref, len_ref, inc_ref, q_ref, tgt_ref, w_ref, pred_ref, acc_ref):
    t = pl.program_id(0)

    @pl.when(t == 0)
    def _():
        acc_ref[...] = jnp.zeros_like(acc_ref)

    hidden = None
    for k in range(pair_count):
        p = pb_ref[t * pair_count + k]
        term = jnp.dot(len_ref[0, k], inc_ref[p], preferred_element_type=F32)
        hidden = term if hidden is None else hidden + term
    q = q_ref[0]
    pred_row = jnp.sum((hidden * q).T, axis=0, keepdims=True)
    pred_ref[0] = pred_row
    err_row = w_ref[0] * (pred_row - tgt_ref[0])
    err_col = jnp.broadcast_to(err_row, q.shape).T
    scaled = (err_col * q).astype(BF16)
    for k in range(pair_count):
        p = pb_ref[t * pair_count + k]
        acc_ref[p] += lax.dot_general(len_ref[0, k], scaled, TN, preferred_element_type=F32)


def trip_pass(pair_flat, lengths, incoming, query, tgt, wts):
    trip_blocks, pair_count, block, rank = lengths.shape
    slots = incoming.shape[0]
    const3 = lambda t, pb: (0, 0, 0)
    return pl.pallas_call(
        functools.partial(trip_kernel, pair_count),
        grid_spec=pltpu.PrefetchScalarGridSpec(
            num_scalar_prefetch=1,
            grid=(trip_blocks,),
            in_specs=[
                pl.BlockSpec((1, pair_count, block, block), lambda t, pb: (t, 0, 0, 0)),
                pl.BlockSpec((slots, block, rank), const3, pipeline_mode=pl.Buffered(1)),
                pl.BlockSpec((1, block, rank), lambda t, pb: (t, 0, 0)),
                pl.BlockSpec((1, 1, block), lambda t, pb: (t, 0, 0)),
                pl.BlockSpec((1, 1, block), lambda t, pb: (t, 0, 0)),
            ],
            out_specs=[
                pl.BlockSpec((1, 1, block), lambda t, pb: (t, 0, 0)),
                pl.BlockSpec((slots, block, rank), const3, pipeline_mode=pl.Buffered(1)),
            ],
        ),
        out_shape=[
            jax.ShapeDtypeStruct((trip_blocks, 1, block), F32),
            jax.ShapeDtypeStruct((slots, block, rank), F32),
        ],
        compiler_params=pltpu.CompilerParams(
            dimension_semantics=("arbitrary",), vmem_limit_bytes=60 * 1024 * 1024
        ),
    )(pair_flat, lengths, incoming, query, tgt, wts)


def smooth_kernel(ext_ref, nb_ref, w_ref, out_ref):
    i = pl.program_id(0)
    rows = out_ref.shape[0]
    span = 3 * rows
    base = i * rows
    window = ext_ref[pl.ds(pl.multiple_of(base, rows), span), :]
    col = lax.broadcasted_iota(jnp.int32, (rows, span), 1)
    own = lax.broadcasted_iota(jnp.int32, (rows, span), 0) + rows
    band = jnp.zeros((rows, span), F32)
    for k in range(nb_ref.shape[1]):
        rel = nb_ref[:, k : k + 1] - base
        wk = w_ref[:, k : k + 1]
        band = band + jnp.where(col == own, wk, 0.0) - jnp.where(col == rel, wk, 0.0)
    hi = band.astype(BF16)
    lo = (band - hi.astype(F32)).astype(BF16)
    out_ref[...] = jnp.dot(hi, window, preferred_element_type=F32) + jnp.dot(
        lo, window, preferred_element_type=F32
    )


def smooth_pass(extended, nb_t, w_t):
    seg_rows = nb_t.shape[0]
    rank = extended.shape[1]
    rows = 128
    return pl.pallas_call(
        smooth_kernel,
        grid=(seg_rows // rows,),
        in_specs=[
            pl.BlockSpec(extended.shape, lambda i: (0, 0), pipeline_mode=pl.Buffered(1)),
            pl.BlockSpec((rows, nb_t.shape[1]), lambda i: (i, 0)),
            pl.BlockSpec((rows, w_t.shape[1]), lambda i: (i, 0)),
        ],
        out_specs=pl.BlockSpec((rows, rank), lambda i: (i, 0)),
        out_shape=jax.ShapeDtypeStruct((seg_rows, rank), F32),
        compiler_params=pltpu.CompilerParams(dimension_semantics=("arbitrary",)),
    )(extended, nb_t, w_t)


def local(
    emb, lengths, pair_block, feats, proj, targets, trip_weight, send_list, nb_index, nb_weight
):
    block_size = lengths.shape[2]
    rank_width = emb.shape[1]
    seg_rows = emb.shape[0]
    block_count = seg_rows // block_size
    regions = lax.axis_size("region")
    blocks = emb.reshape(block_count, block_size, rank_width)
    send_rows = send_list[0, 0]
    live_mask = send_rows >= 0
    slot_count = send_rows.shape[1]
    outgoing = blocks[jnp.where(live_mask, send_rows, 0)]
    incoming = lax.all_to_all(outgoing, "region", split_axis=0, concat_axis=0, tiled=True)
    incoming = incoming.reshape(regions * slot_count, block_size, rank_width)
    trip_blocks = lengths.shape[0]
    trip_query = jnp.einsum("ft,fr->tr", feats, proj, preferred_element_type=jnp.float32)
    query_blocks = trip_query.reshape(trip_blocks, block_size, rank_width)

    pred_rows, slot_grad = trip_pass(
        pair_block.reshape(-1),
        lengths,
        incoming,
        query_blocks,
        targets.reshape(trip_blocks, 1, block_size),
        trip_weight.reshape(trip_blocks, 1, block_size),
    )
    predicted = pred_rows.reshape(trip_blocks * block_size)

    returned = lax.all_to_all(
        slot_grad.reshape(regions, slot_count, block_size, rank_width),
        "region",
        split_axis=0,
        concat_axis=0,
        tiled=True,
    )
    returned = returned.reshape(regions * slot_count, block_size * rank_width)
    target_rows = jnp.where(live_mask, send_rows, -1).reshape(-1)
    onehot = (target_rows[None, :] == jnp.arange(block_count, dtype=jnp.int32)[:, None]).astype(F32)
    owned = jnp.dot(onehot, returned, precision=lax.Precision.HIGHEST, preferred_element_type=F32)
    owned = owned.reshape(seg_rows, rank_width)

    extended = with_halo(emb, (("region", 0),), block_size)
    smoothed = smooth_pass(extended, nb_index[0].T, nb_weight[0].T)
    gradient = lax.psum(owned, "rep") + LAM * smoothed
    return (predicted, gradient.astype(jnp.bfloat16))


def solution(mesh):
    placed = (
        P("region", None),
        P(("region", "rep"), None, None, None),
        P(("region", "rep"), None),
        P(None, ("region", "rep")),
        P(),
        P(("region", "rep")),
        P(("region", "rep")),
        P("region", "rep", None, None),
        P("region", None, None),
        P("region", None, None),
    )
    return jax.shard_map(
        local,
        mesh=mesh,
        in_specs=placed,
        out_specs=(P(("region", "rep")), P("region", None)),
        check_vma=False,
    )
```

```python
import functools

import jax
import jax.numpy as jnp
from jax import lax
from jax.experimental import pallas as pl
from jax.experimental.pallas import tpu as pltpu
from jax.sharding import PartitionSpec as P

LAM = 0.25
F32 = jnp.float32
BF16 = jnp.bfloat16


def trip_kernel(pair_count, pb_ref, len_ref, inc_ref, qt_ref, tgt_ref, w_ref, pred_ref, acc_ref):
    t = pl.program_id(0)

    @pl.when(t == 0)
    def _():
        acc_ref[...] = jnp.zeros_like(acc_ref)

    hidden = None
    for k in range(pair_count):
        p = pb_ref[t * pair_count + k]
        term = jnp.dot(len_ref[0, k], inc_ref[p], preferred_element_type=F32)
        hidden = term if hidden is None else hidden + term
    q_t = qt_ref[...]
    pred_row = jnp.sum(hidden.T * q_t, axis=0, keepdims=True)
    pred_ref[0] = pred_row
    err_row = w_ref[0] * (pred_row - tgt_ref[0])
    scaled_t = (err_row * q_t).astype(BF16)
    for k in range(pair_count):
        p = pb_ref[t * pair_count + k]
        acc_ref[p] += jnp.dot(scaled_t, len_ref[0, k], preferred_element_type=F32)


def trip_pass(pair_flat, lengths, incoming, query_t, tgt, wts):
    trip_blocks, pair_count, block, rank = lengths.shape
    slots = incoming.shape[0]
    const3 = lambda t, pb: (0, 0, 0)
    return pl.pallas_call(
        functools.partial(trip_kernel, pair_count),
        grid_spec=pltpu.PrefetchScalarGridSpec(
            num_scalar_prefetch=1,
            grid=(trip_blocks,),
            in_specs=[
                pl.BlockSpec((1, pair_count, block, block), lambda t, pb: (t, 0, 0, 0)),
                pl.BlockSpec((slots, block, rank), const3, pipeline_mode=pl.Buffered(1)),
                pl.BlockSpec((rank, block), lambda t, pb: (0, t)),
                pl.BlockSpec((1, 1, block), lambda t, pb: (t, 0, 0)),
                pl.BlockSpec((1, 1, block), lambda t, pb: (t, 0, 0)),
            ],
            out_specs=[
                pl.BlockSpec((1, 1, block), lambda t, pb: (t, 0, 0)),
                pl.BlockSpec((slots, block, rank), const3, pipeline_mode=pl.Buffered(1)),
            ],
        ),
        out_shape=[
            jax.ShapeDtypeStruct((trip_blocks, 1, block), F32),
            jax.ShapeDtypeStruct((slots, block, rank), F32),
        ],
        compiler_params=pltpu.CompilerParams(
            dimension_semantics=("arbitrary",), vmem_limit_bytes=60 * 1024 * 1024
        ),
    )(pair_flat, lengths, incoming, query_t, tgt, wts)


def band_of(nb_ref, w_ref, base, rows):
    span = 3 * rows
    col = lax.broadcasted_iota(jnp.int32, (rows, span), 1)
    own = lax.broadcasted_iota(jnp.int32, (rows, span), 0) + rows
    band = jnp.zeros((rows, span), F32)
    for k in range(nb_ref.shape[1]):
        rel = nb_ref[:, k : k + 1] - base
        wk = w_ref[:, k : k + 1]
        band = band + jnp.where(col == own, wk, 0.0) - jnp.where(col == rel, wk, 0.0)
    hi = band.astype(BF16)
    lo = (band - hi.astype(F32)).astype(BF16)
    return hi, lo


def apply_band(hi, lo, window):
    return jnp.dot(hi, window, preferred_element_type=F32) + jnp.dot(
        lo, window, preferred_element_type=F32
    )


def smooth_inner_kernel(emb_ref, nb_ref, w_ref, out_ref):
    rows = out_ref.shape[0]
    i = pl.program_id(0) + 1
    hi, lo = band_of(nb_ref, w_ref, i * rows, rows)
    window = emb_ref[pl.ds(pl.multiple_of((i - 1) * rows, rows), 3 * rows), :]
    out_ref[...] = apply_band(hi, lo, window)


def smooth_edge_kernel(last, win_ref, nb_ref, w_ref, out_ref):
    rows = out_ref.shape[0]
    i = pl.program_id(0) * last
    hi, lo = band_of(nb_ref, w_ref, i * rows, rows)
    out_ref[...] = apply_band(hi, lo, win_ref[0])


def smooth_inner(emb, nb_t, w_t, rows):
    seg_rows, rank = emb.shape
    inner = seg_rows // rows - 2
    return pl.pallas_call(
        smooth_inner_kernel,
        grid=(inner,),
        in_specs=[
            pl.BlockSpec(emb.shape, lambda i: (0, 0), pipeline_mode=pl.Buffered(1)),
            pl.BlockSpec((rows, nb_t.shape[1]), lambda i: (i + 1, 0)),
            pl.BlockSpec((rows, w_t.shape[1]), lambda i: (i + 1, 0)),
        ],
        out_specs=pl.BlockSpec((rows, rank), lambda i: (i, 0)),
        out_shape=jax.ShapeDtypeStruct((inner * rows, rank), F32),
        compiler_params=pltpu.CompilerParams(dimension_semantics=("arbitrary",)),
    )(emb, nb_t, w_t)


def smooth_edge(windows, nb_t, w_t, rows):
    rank = windows.shape[2]
    last = nb_t.shape[0] // rows - 1
    return pl.pallas_call(
        functools.partial(smooth_edge_kernel, last),
        grid=(2,),
        in_specs=[
            pl.BlockSpec((1,) + windows.shape[1:], lambda i: (i, 0, 0)),
            pl.BlockSpec((rows, nb_t.shape[1]), lambda i: (i * last, 0)),
            pl.BlockSpec((rows, w_t.shape[1]), lambda i: (i * last, 0)),
        ],
        out_specs=pl.BlockSpec((rows, rank), lambda i: (i, 0)),
        out_shape=jax.ShapeDtypeStruct((2 * rows, rank), F32),
        compiler_params=pltpu.CompilerParams(dimension_semantics=("arbitrary",)),
    )(windows, nb_t, w_t)


def owned_kernel(tgt_ref, ret_ref, out_ref, acc_ref):
    c = pl.program_id(0)
    chunk = ret_ref.shape[0]

    @pl.when(c == 0)
    def _():
        acc_ref[...] = jnp.zeros_like(acc_ref)

    for s in range(chunk):
        b = tgt_ref[c * chunk + s]

        @pl.when(b >= 0)
        def _():
            acc_ref[b] += ret_ref[s]

    @pl.when(c == pl.num_programs(0) - 1)
    def _():
        for b in range(acc_ref.shape[0]):
            out_ref[b] = acc_ref[b].T


def owned_pass(targets, returned, block_count, chunk=32):
    slots, rank, block = returned.shape
    return pl.pallas_call(
        owned_kernel,
        grid_spec=pltpu.PrefetchScalarGridSpec(
            num_scalar_prefetch=1,
            grid=(slots // chunk,),
            in_specs=[pl.BlockSpec((chunk, rank, block), lambda c, tg: (c, 0, 0))],
            out_specs=pl.BlockSpec(
                (block_count, block, rank), lambda c, tg: (0, 0, 0), pipeline_mode=pl.Buffered(1)
            ),
            scratch_shapes=[pltpu.VMEM((block_count, rank, block), F32)],
        ),
        out_shape=jax.ShapeDtypeStruct((block_count, block, rank), F32),
        compiler_params=pltpu.CompilerParams(dimension_semantics=("arbitrary",)),
    )(targets, returned)


def local(
    emb, lengths, pair_block, feats, proj, targets, trip_weight, send_list, nb_index, nb_weight
):
    block_size = lengths.shape[2]
    rank_width = emb.shape[1]
    seg_rows = emb.shape[0]
    block_count = seg_rows // block_size
    regions = lax.axis_size("region")
    blocks = emb.reshape(block_count, block_size, rank_width)
    send_rows = send_list[0, 0]
    live_mask = send_rows >= 0
    slot_count = send_rows.shape[1]
    outgoing = blocks[jnp.where(live_mask, send_rows, 0)]
    incoming = lax.all_to_all(outgoing, "region", split_axis=0, concat_axis=0, tiled=True)
    incoming = incoming.reshape(regions * slot_count, block_size, rank_width)
    trip_blocks = lengths.shape[0]
    query_t = jnp.einsum("fr,ft->rt", proj, feats, preferred_element_type=F32)

    nb_t = nb_index[0].T
    w_t = nb_weight[0].T
    inner = smooth_inner(emb, nb_t, w_t, block_size)

    pred_rows, slot_grad = trip_pass(
        pair_block.reshape(-1),
        lengths,
        incoming,
        query_t,
        targets.reshape(trip_blocks, 1, block_size),
        trip_weight.reshape(trip_blocks, 1, block_size),
    )
    predicted = pred_rows.reshape(trip_blocks * block_size)

    returned = lax.all_to_all(
        slot_grad.reshape(regions, slot_count, rank_width, block_size),
        "region",
        split_axis=0,
        concat_axis=0,
        tiled=True,
    )
    returned = returned.reshape(regions * slot_count, rank_width, block_size)

    count = regions
    head = emb[:block_size]
    tail = emb[seg_rows - block_size :]
    prev_tail = lax.ppermute(tail, "region", [(i, (i + 1) % count) for i in range(count)])
    next_head = lax.ppermute(head, "region", [((i + 1) % count, i) for i in range(count)])
    windows = jnp.stack(
        [
            jnp.concatenate([prev_tail, emb[: 2 * block_size]], axis=0),
            jnp.concatenate([emb[seg_rows - 2 * block_size :], next_head], axis=0),
        ]
    )
    edge = smooth_edge(windows, nb_t, w_t, block_size)
    smoothed = jnp.concatenate([edge[:block_size], inner, edge[block_size:]], axis=0)

    target_rows = jnp.where(live_mask, send_rows, -1).reshape(-1)
    owned = owned_pass(target_rows, returned, block_count).reshape(seg_rows, rank_width)
    partner = lax.ppermute(owned, "rep", [(0, 1), (1, 0)])
    gradient = (owned + partner) + LAM * smoothed
    return (predicted, gradient.astype(jnp.bfloat16))


def solution(mesh):
    placed = (
        P("region", None),
        P(("region", "rep"), None, None, None),
        P(("region", "rep"), None),
        P(None, ("region", "rep")),
        P(),
        P(("region", "rep")),
        P(("region", "rep")),
        P("region", "rep", None, None),
        P("region", None, None),
        P("region", None, None),
    )
    return jax.shard_map(
        local,
        mesh=mesh,
        in_specs=placed,
        out_specs=(P(("region", "rep")), P("region", None)),
        check_vma=False,
    )
```

```python
import functools

import jax
import jax.numpy as jnp
from jax import lax
from jax.experimental import pallas as pl
from jax.experimental.pallas import tpu as pltpu
from jax.sharding import PartitionSpec as P

LAM = 0.25
F32 = jnp.float32
BF16 = jnp.bfloat16


def trip_kernel(
    pair_count, pb_ref, len_ref, inc_ref, qt_ref, tgt_ref, w_ref, pred_ref, out_ref, acc_ref
):
    t = pl.program_id(0)

    @pl.when(t == 0)
    def _():
        acc_ref[...] = jnp.zeros_like(acc_ref)

    hidden = None
    for k in range(pair_count):
        p = pb_ref[t * pair_count + k]
        term = jnp.dot(len_ref[0, k], inc_ref[p], preferred_element_type=F32)
        hidden = term if hidden is None else hidden + term
    q_t = qt_ref[...]
    pred_row = jnp.sum(hidden.T * q_t, axis=0, keepdims=True)
    pred_ref[0] = pred_row
    err_row = w_ref[0] * (pred_row - tgt_ref[0])
    scaled_t = (err_row * q_t).astype(BF16)
    for k in range(pair_count):
        p = pb_ref[t * pair_count + k]
        acc_ref[p] += jnp.dot(scaled_t, len_ref[0, k], preferred_element_type=F32)

    @pl.when(t == pl.num_programs(0) - 1)
    def _():
        out_ref[...] = acc_ref[...].astype(out_ref.dtype)


def trip_pass(pair_flat, lengths, incoming, query_t, tgt, wts):
    trip_blocks, pair_count, block, rank = lengths.shape
    slots = incoming.shape[0]
    const3 = lambda t, pb: (0, 0, 0)
    return pl.pallas_call(
        functools.partial(trip_kernel, pair_count),
        grid_spec=pltpu.PrefetchScalarGridSpec(
            num_scalar_prefetch=1,
            grid=(trip_blocks,),
            in_specs=[
                pl.BlockSpec((1, pair_count, block, block), lambda t, pb: (t, 0, 0, 0)),
                pl.BlockSpec((slots, block, rank), const3, pipeline_mode=pl.Buffered(1)),
                pl.BlockSpec((rank, block), lambda t, pb: (0, t)),
                pl.BlockSpec((1, 1, block), lambda t, pb: (t, 0, 0)),
                pl.BlockSpec((1, 1, block), lambda t, pb: (t, 0, 0)),
            ],
            out_specs=[
                pl.BlockSpec((1, 1, block), lambda t, pb: (t, 0, 0)),
                pl.BlockSpec((slots, block, rank), const3, pipeline_mode=pl.Buffered(1)),
            ],
            scratch_shapes=[pltpu.VMEM((slots, block, rank), F32)],
        ),
        out_shape=[
            jax.ShapeDtypeStruct((trip_blocks, 1, block), F32),
            jax.ShapeDtypeStruct((slots, block, rank), BF16),
        ],
        compiler_params=pltpu.CompilerParams(
            dimension_semantics=("arbitrary",), vmem_limit_bytes=60 * 1024 * 1024
        ),
    )(pair_flat, lengths, incoming, query_t, tgt, wts)


def band_of(nb_ref, w_ref, base, rows):
    span = 3 * rows
    col = lax.broadcasted_iota(jnp.int32, (rows, span), 1)
    own = lax.broadcasted_iota(jnp.int32, (rows, span), 0) + rows
    band = jnp.zeros((rows, span), F32)
    for k in range(nb_ref.shape[1]):
        rel = nb_ref[:, k : k + 1] - base
        wk = w_ref[:, k : k + 1]
        band = band + jnp.where(col == own, wk, 0.0) - jnp.where(col == rel, wk, 0.0)
    hi = band.astype(BF16)
    lo = (band - hi.astype(F32)).astype(BF16)
    return hi, lo


def apply_band(hi, lo, window):
    return jnp.dot(hi, window, preferred_element_type=F32) + jnp.dot(
        lo, window, preferred_element_type=F32
    )


def smooth_inner_kernel(emb_ref, nb_ref, w_ref, out_ref):
    rows = out_ref.shape[0]
    i = pl.program_id(0) + 1
    hi, lo = band_of(nb_ref, w_ref, i * rows, rows)
    window = emb_ref[pl.ds(pl.multiple_of((i - 1) * rows, rows), 3 * rows), :]
    out_ref[...] = apply_band(hi, lo, window)


def smooth_edge_kernel(last, win_ref, nb_ref, w_ref, out_ref):
    rows = out_ref.shape[0]
    i = pl.program_id(0) * last
    hi, lo = band_of(nb_ref, w_ref, i * rows, rows)
    out_ref[...] = apply_band(hi, lo, win_ref[0])


def smooth_inner(emb, nb_t, w_t, rows):
    seg_rows, rank = emb.shape
    inner = seg_rows // rows - 2
    return pl.pallas_call(
        smooth_inner_kernel,
        grid=(inner,),
        in_specs=[
            pl.BlockSpec(emb.shape, lambda i: (0, 0), pipeline_mode=pl.Buffered(1)),
            pl.BlockSpec((rows, nb_t.shape[1]), lambda i: (i + 1, 0)),
            pl.BlockSpec((rows, w_t.shape[1]), lambda i: (i + 1, 0)),
        ],
        out_specs=pl.BlockSpec((rows, rank), lambda i: (i, 0)),
        out_shape=jax.ShapeDtypeStruct((inner * rows, rank), F32),
        compiler_params=pltpu.CompilerParams(dimension_semantics=("arbitrary",)),
    )(emb, nb_t, w_t)


def smooth_edge(windows, nb_t, w_t, rows):
    rank = windows.shape[2]
    last = nb_t.shape[0] // rows - 1
    return pl.pallas_call(
        functools.partial(smooth_edge_kernel, last),
        grid=(2,),
        in_specs=[
            pl.BlockSpec((1,) + windows.shape[1:], lambda i: (i, 0, 0)),
            pl.BlockSpec((rows, nb_t.shape[1]), lambda i: (i * last, 0)),
            pl.BlockSpec((rows, w_t.shape[1]), lambda i: (i * last, 0)),
        ],
        out_specs=pl.BlockSpec((rows, rank), lambda i: (i, 0)),
        out_shape=jax.ShapeDtypeStruct((2 * rows, rank), F32),
        compiler_params=pltpu.CompilerParams(dimension_semantics=("arbitrary",)),
    )(windows, nb_t, w_t)


def owned_kernel(tgt_ref, ret_ref, out_ref, acc_ref):
    c = pl.program_id(0)
    chunk = ret_ref.shape[0]

    @pl.when(c == 0)
    def _():
        acc_ref[...] = jnp.zeros_like(acc_ref)

    for s in range(chunk):
        b = tgt_ref[c * chunk + s]

        @pl.when(b >= 0)
        def _():
            acc_ref[b] += ret_ref[s].astype(F32)

    @pl.when(c == pl.num_programs(0) - 1)
    def _():
        for b in range(acc_ref.shape[0]):
            out_ref[b] = acc_ref[b].T


def owned_pass(targets, returned, block_count, chunk=32):
    slots, rank, block = returned.shape
    return pl.pallas_call(
        owned_kernel,
        grid_spec=pltpu.PrefetchScalarGridSpec(
            num_scalar_prefetch=1,
            grid=(slots // chunk,),
            in_specs=[pl.BlockSpec((chunk, rank, block), lambda c, tg: (c, 0, 0))],
            out_specs=pl.BlockSpec(
                (block_count, block, rank), lambda c, tg: (0, 0, 0), pipeline_mode=pl.Buffered(1)
            ),
            scratch_shapes=[pltpu.VMEM((block_count, rank, block), F32)],
        ),
        out_shape=jax.ShapeDtypeStruct((block_count, block, rank), F32),
        compiler_params=pltpu.CompilerParams(dimension_semantics=("arbitrary",)),
    )(targets, returned)


def local(
    emb, lengths, pair_block, feats, proj, targets, trip_weight, send_list, nb_index, nb_weight
):
    block_size = lengths.shape[2]
    rank_width = emb.shape[1]
    seg_rows = emb.shape[0]
    block_count = seg_rows // block_size
    regions = lax.axis_size("region")
    blocks = emb.reshape(block_count, block_size, rank_width)
    send_rows = send_list[0, 0]
    live_mask = send_rows >= 0
    slot_count = send_rows.shape[1]
    outgoing = blocks[jnp.where(live_mask, send_rows, 0)]
    incoming = lax.all_to_all(outgoing, "region", split_axis=0, concat_axis=0, tiled=True)
    incoming = incoming.reshape(regions * slot_count, block_size, rank_width)
    trip_blocks = lengths.shape[0]
    query_t = jnp.einsum("fr,ft->rt", proj, feats, preferred_element_type=F32)

    nb_t = nb_index[0].T
    w_t = nb_weight[0].T
    inner = smooth_inner(emb, nb_t, w_t, block_size)

    pred_rows, slot_grad = trip_pass(
        pair_block.reshape(-1),
        lengths,
        incoming,
        query_t,
        targets.reshape(trip_blocks, 1, block_size),
        trip_weight.reshape(trip_blocks, 1, block_size),
    )
    predicted = pred_rows.reshape(trip_blocks * block_size)

    returned = lax.all_to_all(
        slot_grad.reshape(regions, slot_count, rank_width, block_size),
        "region",
        split_axis=0,
        concat_axis=0,
        tiled=True,
    )
    returned = returned.reshape(regions * slot_count, rank_width, block_size)

    count = regions
    head = emb[:block_size]
    tail = emb[seg_rows - block_size :]
    prev_tail = lax.ppermute(tail, "region", [(i, (i + 1) % count) for i in range(count)])
    next_head = lax.ppermute(head, "region", [((i + 1) % count, i) for i in range(count)])
    windows = jnp.stack(
        [
            jnp.concatenate([prev_tail, emb[: 2 * block_size]], axis=0),
            jnp.concatenate([emb[seg_rows - 2 * block_size :], next_head], axis=0),
        ]
    )
    edge = smooth_edge(windows, nb_t, w_t, block_size)
    smoothed = jnp.concatenate([edge[:block_size], inner, edge[block_size:]], axis=0)

    target_rows = jnp.where(live_mask, send_rows, -1).reshape(-1)
    owned = owned_pass(target_rows, returned, block_count).reshape(seg_rows, rank_width)
    partner = lax.ppermute(owned, "rep", [(0, 1), (1, 0)])
    gradient = (owned + partner) + LAM * smoothed
    return (predicted, gradient.astype(jnp.bfloat16))


def solution(mesh):
    placed = (
        P("region", None),
        P(("region", "rep"), None, None, None),
        P(("region", "rep"), None),
        P(None, ("region", "rep")),
        P(),
        P(("region", "rep")),
        P(("region", "rep")),
        P("region", "rep", None, None),
        P("region", None, None),
        P("region", None, None),
    )
    return jax.shard_map(
        local,
        mesh=mesh,
        in_specs=placed,
        out_specs=(P(("region", "rep")), P("region", None)),
        check_vma=False,
    )
```

```python
import functools

import jax
import jax.numpy as jnp
from jax import lax
from jax.experimental import pallas as pl
from jax.experimental.pallas import tpu as pltpu
from jax.sharding import PartitionSpec as P

LAM = 0.25
F32 = jnp.float32
BF16 = jnp.bfloat16
TN = (((0,), (0,)), ((), ()))


def trip_kernel(
    pair_count, pb_ref, len_ref, inc_ref, qt_ref, tgt_ref, w_ref, _, pred_ref, out_ref, acc_ref
):
    t = pl.program_id(0)

    @pl.when(t == 0)
    def _():
        acc_ref[...] = jnp.zeros_like(acc_ref)

    hidden = None
    for k in range(pair_count):
        p = pb_ref[t * pair_count + k]
        term = jnp.dot(len_ref[0, k], inc_ref[p], preferred_element_type=F32)
        hidden = term if hidden is None else hidden + term
    q_t = qt_ref[...]
    pred_row = jnp.sum(hidden.T * q_t, axis=0, keepdims=True)
    pred_ref[0] = pred_row
    err_row = w_ref[0] * (pred_row - tgt_ref[0])
    scaled_t = (err_row * q_t).astype(BF16)
    for k in range(pair_count):
        p = pb_ref[t * pair_count + k]
        acc_ref[p] += jnp.dot(scaled_t, len_ref[0, k], preferred_element_type=F32)

    @pl.when(t == pl.num_programs(0) - 1)
    def _():
        out_ref[...] = acc_ref[...].astype(out_ref.dtype)


def trip_pass(pair_flat, lengths, incoming, query_t, tgt, wts, after):
    trip_blocks, pair_count, block, rank = lengths.shape
    slots = incoming.shape[0]
    const3 = lambda t, pb: (0, 0, 0)
    return pl.pallas_call(
        functools.partial(trip_kernel, pair_count),
        grid_spec=pltpu.PrefetchScalarGridSpec(
            num_scalar_prefetch=1,
            grid=(trip_blocks,),
            in_specs=[
                pl.BlockSpec((1, pair_count, block, block), lambda t, pb: (t, 0, 0, 0)),
                pl.BlockSpec((slots, block, rank), const3, pipeline_mode=pl.Buffered(1)),
                pl.BlockSpec((rank, block), lambda t, pb: (0, t)),
                pl.BlockSpec((1, 1, block), lambda t, pb: (t, 0, 0)),
                pl.BlockSpec((1, 1, block), lambda t, pb: (t, 0, 0)),
                pl.BlockSpec(memory_space=pl.ANY),
            ],
            out_specs=[
                pl.BlockSpec((1, 1, block), lambda t, pb: (t, 0, 0)),
                pl.BlockSpec((slots, block, rank), const3, pipeline_mode=pl.Buffered(1)),
            ],
            scratch_shapes=[pltpu.VMEM((slots, block, rank), F32)],
        ),
        out_shape=[
            jax.ShapeDtypeStruct((trip_blocks, 1, block), F32),
            jax.ShapeDtypeStruct((slots, block, rank), BF16),
        ],
        compiler_params=pltpu.CompilerParams(
            dimension_semantics=("arbitrary",), vmem_limit_bytes=60 * 1024 * 1024
        ),
    )(pair_flat, lengths, incoming, query_t, tgt, wts, after)


def band_of(nb_ref, w_ref, base, rows):
    span = 3 * rows
    row = lax.broadcasted_iota(jnp.int32, (span, rows), 0)
    band = jnp.zeros((span, rows), F32)
    for k in range(nb_ref.shape[0]):
        rel = nb_ref[k : k + 1, :] - base
        band = band - jnp.where(row == rel, w_ref[k : k + 1, :], 0.0)
    mid_row = lax.broadcasted_iota(jnp.int32, (rows, rows), 0)
    mid_col = lax.broadcasted_iota(jnp.int32, (rows, rows), 1)
    total = jnp.sum(w_ref[...], axis=0, keepdims=True)
    mid = band[rows : 2 * rows] + jnp.where(mid_row == mid_col, total, 0.0)
    band = jnp.concatenate([band[:rows], mid, band[2 * rows :]], axis=0)
    hi = band.astype(BF16)
    lo = (band - hi.astype(F32)).astype(BF16)
    return hi, lo


def apply_band(hi, lo, window):
    return lax.dot_general(hi, window, TN, preferred_element_type=F32) + lax.dot_general(
        lo, window, TN, preferred_element_type=F32
    )


def smooth_inner_kernel(emb_ref, nb_ref, w_ref, out_ref):
    rows = out_ref.shape[0]
    i = pl.program_id(0) + 1
    hi, lo = band_of(nb_ref, w_ref, i * rows, rows)
    window = emb_ref[pl.ds(pl.multiple_of((i - 1) * rows, rows), 3 * rows), :]
    out_ref[...] = apply_band(hi, lo, window)


def smooth_edge_kernel(last, win_ref, nb_ref, w_ref, out_ref):
    rows = out_ref.shape[0]
    i = pl.program_id(0) * last
    hi, lo = band_of(nb_ref, w_ref, i * rows, rows)
    out_ref[...] = apply_band(hi, lo, win_ref[0])


def smooth_inner(emb, nb_t, w_t, rows):
    seg_rows, rank = emb.shape
    inner = seg_rows // rows - 2
    return pl.pallas_call(
        smooth_inner_kernel,
        grid=(inner,),
        in_specs=[
            pl.BlockSpec(emb.shape, lambda i: (0, 0), pipeline_mode=pl.Buffered(1)),
            pl.BlockSpec((nb_t.shape[0], rows), lambda i: (0, i + 1)),
            pl.BlockSpec((w_t.shape[0], rows), lambda i: (0, i + 1)),
        ],
        out_specs=pl.BlockSpec((rows, rank), lambda i: (i, 0)),
        out_shape=jax.ShapeDtypeStruct((inner * rows, rank), F32),
        compiler_params=pltpu.CompilerParams(dimension_semantics=("arbitrary",)),
    )(emb, nb_t, w_t)


def smooth_edge(windows, nb_t, w_t, rows):
    rank = windows.shape[2]
    last = nb_t.shape[1] // rows - 1
    return pl.pallas_call(
        functools.partial(smooth_edge_kernel, last),
        grid=(2,),
        in_specs=[
            pl.BlockSpec((1,) + windows.shape[1:], lambda i: (i, 0, 0)),
            pl.BlockSpec((nb_t.shape[0], rows), lambda i: (0, i * last)),
            pl.BlockSpec((w_t.shape[0], rows), lambda i: (0, i * last)),
        ],
        out_specs=pl.BlockSpec((rows, rank), lambda i: (i, 0)),
        out_shape=jax.ShapeDtypeStruct((2 * rows, rank), F32),
        compiler_params=pltpu.CompilerParams(dimension_semantics=("arbitrary",)),
    )(windows, nb_t, w_t)


def owned_kernel(tgt_ref, ret_ref, out_ref, acc_ref):
    c = pl.program_id(0)
    chunk = ret_ref.shape[0]

    @pl.when(c == 0)
    def _():
        acc_ref[...] = jnp.zeros_like(acc_ref)

    for s in range(chunk):
        b = tgt_ref[c * chunk + s]

        @pl.when(b >= 0)
        def _():
            acc_ref[b] += ret_ref[s].astype(F32)

    @pl.when(c == pl.num_programs(0) - 1)
    def _():
        for b in range(acc_ref.shape[0]):
            out_ref[b] = acc_ref[b].T


def owned_pass(targets, returned, block_count, chunk=32):
    slots, rank, block = returned.shape
    return pl.pallas_call(
        owned_kernel,
        grid_spec=pltpu.PrefetchScalarGridSpec(
            num_scalar_prefetch=1,
            grid=(slots // chunk,),
            in_specs=[pl.BlockSpec((chunk, rank, block), lambda c, tg: (c, 0, 0))],
            out_specs=pl.BlockSpec(
                (block_count, block, rank), lambda c, tg: (0, 0, 0), pipeline_mode=pl.Buffered(1)
            ),
            scratch_shapes=[pltpu.VMEM((block_count, rank, block), F32)],
        ),
        out_shape=jax.ShapeDtypeStruct((block_count, block, rank), F32),
        compiler_params=pltpu.CompilerParams(dimension_semantics=("arbitrary",)),
    )(targets, returned)


def local(
    emb, lengths, pair_block, feats, proj, targets, trip_weight, send_list, nb_index, nb_weight
):
    block_size = lengths.shape[2]
    rank_width = emb.shape[1]
    seg_rows = emb.shape[0]
    block_count = seg_rows // block_size
    regions = lax.axis_size("region")
    blocks = emb.reshape(block_count, block_size, rank_width)
    send_rows = send_list[0, 0]
    live_mask = send_rows >= 0
    slot_count = send_rows.shape[1]
    outgoing = blocks[jnp.where(live_mask, send_rows, 0)]
    incoming = lax.all_to_all(outgoing, "region", split_axis=0, concat_axis=0, tiled=True)
    incoming = incoming.reshape(regions * slot_count, block_size, rank_width)
    trip_blocks = lengths.shape[0]
    query_t = jnp.einsum("fr,ft->rt", proj, feats, preferred_element_type=F32)

    nb_t = nb_index[0]
    w_t = nb_weight[0]
    inner = smooth_inner(emb, nb_t, w_t, block_size)
    count = regions
    head = emb[:block_size]
    tail = emb[seg_rows - block_size :]
    prev_tail = lax.ppermute(tail, "region", [(i, (i + 1) % count) for i in range(count)])
    next_head = lax.ppermute(head, "region", [((i + 1) % count, i) for i in range(count)])
    windows = jnp.stack(
        [
            jnp.concatenate([prev_tail, emb[: 2 * block_size]], axis=0),
            jnp.concatenate([emb[seg_rows - 2 * block_size :], next_head], axis=0),
        ]
    )
    edge = smooth_edge(windows, nb_t, w_t, block_size)
    smoothed = jnp.concatenate([edge[:block_size], inner, edge[block_size:]], axis=0)

    pred_rows, slot_grad = trip_pass(
        pair_block.reshape(-1),
        lengths,
        incoming,
        query_t,
        targets.reshape(trip_blocks, 1, block_size),
        trip_weight.reshape(trip_blocks, 1, block_size),
        smoothed,
    )
    predicted = pred_rows.reshape(trip_blocks * block_size)

    returned = lax.all_to_all(
        slot_grad.reshape(regions, slot_count, rank_width, block_size),
        "region",
        split_axis=0,
        concat_axis=0,
        tiled=True,
    )
    returned = returned.reshape(regions * slot_count, rank_width, block_size)

    target_rows = jnp.where(live_mask, send_rows, -1).reshape(-1)
    owned = owned_pass(target_rows, returned, block_count).reshape(seg_rows, rank_width)
    partner = lax.ppermute(owned, "rep", [(0, 1), (1, 0)])
    gradient = (owned + partner) + LAM * smoothed
    return (predicted, gradient.astype(jnp.bfloat16))


def solution(mesh):
    placed = (
        P("region", None),
        P(("region", "rep"), None, None, None),
        P(("region", "rep"), None),
        P(None, ("region", "rep")),
        P(),
        P(("region", "rep")),
        P(("region", "rep")),
        P("region", "rep", None, None),
        P("region", None, None),
        P("region", None, None),
    )
    return jax.shard_map(
        local,
        mesh=mesh,
        in_specs=placed,
        out_specs=(P(("region", "rep")), P("region", None)),
        check_vma=False,
    )
```

```python
import functools

import jax
import jax.numpy as jnp
from jax import lax
from jax.experimental import pallas as pl
from jax.experimental.pallas import tpu as pltpu
from jax.sharding import PartitionSpec as P

LAM = 0.25
F32 = jnp.float32
BF16 = jnp.bfloat16
TN = (((0,), (0,)), ((), ()))


def trip_kernel(
    pair_count, pb_ref, len_ref, inc_ref, qt_ref, tgt_ref, w_ref, _, pred_ref, out_ref, acc_ref
):
    t = pl.program_id(0)

    @pl.when(t == 0)
    def _():
        acc_ref[...] = jnp.zeros_like(acc_ref)

    hidden = None
    for k in range(0, pair_count, 2):
        p0 = pb_ref[t * pair_count + k]
        p1 = pb_ref[t * pair_count + k + 1]
        lhs = jnp.concatenate([len_ref[0, k], len_ref[0, k + 1]], axis=1)
        rhs = jnp.concatenate([inc_ref[p0], inc_ref[p1]], axis=0)
        term = jnp.dot(lhs, rhs, preferred_element_type=F32)
        hidden = term if hidden is None else hidden + term
    q_t = qt_ref[...]
    pred_row = jnp.sum(hidden.T * q_t, axis=0, keepdims=True)
    pred_ref[0] = pred_row
    err_row = w_ref[0] * (pred_row - tgt_ref[0])
    scaled_t = (err_row * q_t).astype(BF16)
    block = q_t.shape[1]
    for k in range(0, pair_count, 2):
        p0 = pb_ref[t * pair_count + k]
        p1 = pb_ref[t * pair_count + k + 1]
        rhs = jnp.concatenate([len_ref[0, k], len_ref[0, k + 1]], axis=1)
        both = jnp.dot(scaled_t, rhs, preferred_element_type=F32)
        acc_ref[p0] += both[:, :block]
        acc_ref[p1] += both[:, block:]

    @pl.when(t == pl.num_programs(0) - 1)
    def _():
        out_ref[...] = acc_ref[...].astype(out_ref.dtype)


def trip_pass(pair_flat, lengths, incoming, query_t, tgt, wts, after):
    trip_blocks, pair_count, block, rank = lengths.shape
    slots = incoming.shape[0]
    const3 = lambda t, pb: (0, 0, 0)
    return pl.pallas_call(
        functools.partial(trip_kernel, pair_count),
        grid_spec=pltpu.PrefetchScalarGridSpec(
            num_scalar_prefetch=1,
            grid=(trip_blocks,),
            in_specs=[
                pl.BlockSpec((1, pair_count, block, block), lambda t, pb: (t, 0, 0, 0)),
                pl.BlockSpec((slots, block, rank), const3, pipeline_mode=pl.Buffered(1)),
                pl.BlockSpec((rank, block), lambda t, pb: (0, t)),
                pl.BlockSpec((1, 1, block), lambda t, pb: (t, 0, 0)),
                pl.BlockSpec((1, 1, block), lambda t, pb: (t, 0, 0)),
                pl.BlockSpec(memory_space=pl.ANY),
            ],
            out_specs=[
                pl.BlockSpec((1, 1, block), lambda t, pb: (t, 0, 0)),
                pl.BlockSpec((slots, block, rank), const3, pipeline_mode=pl.Buffered(1)),
            ],
            scratch_shapes=[pltpu.VMEM((slots, block, rank), F32)],
        ),
        out_shape=[
            jax.ShapeDtypeStruct((trip_blocks, 1, block), F32),
            jax.ShapeDtypeStruct((slots, block, rank), BF16),
        ],
        compiler_params=pltpu.CompilerParams(
            dimension_semantics=("arbitrary",), vmem_limit_bytes=60 * 1024 * 1024
        ),
    )(pair_flat, lengths, incoming, query_t, tgt, wts, after)


def band_of(nb_ref, w_ref, base, rows):
    span = 3 * rows
    row = lax.broadcasted_iota(jnp.int32, (span, rows), 0)
    band = jnp.zeros((span, rows), F32)
    for k in range(nb_ref.shape[0]):
        rel = nb_ref[k : k + 1, :] - base
        band = band - jnp.where(row == rel, w_ref[k : k + 1, :], 0.0)
    mid_row = lax.broadcasted_iota(jnp.int32, (rows, rows), 0)
    mid_col = lax.broadcasted_iota(jnp.int32, (rows, rows), 1)
    total = jnp.sum(w_ref[...], axis=0, keepdims=True)
    mid = band[rows : 2 * rows] + jnp.where(mid_row == mid_col, total, 0.0)
    band = jnp.concatenate([band[:rows], mid, band[2 * rows :]], axis=0)
    hi = band.astype(BF16)
    lo = (band - hi.astype(F32)).astype(BF16)
    return hi, lo


def apply_band(hi, lo, window):
    return lax.dot_general(hi, window, TN, preferred_element_type=F32) + lax.dot_general(
        lo, window, TN, preferred_element_type=F32
    )


def smooth_inner_kernel(emb_ref, nb_ref, w_ref, out_ref):
    rows = out_ref.shape[0]
    i = pl.program_id(0) + 1
    hi, lo = band_of(nb_ref, w_ref, i * rows, rows)
    window = emb_ref[pl.ds(pl.multiple_of((i - 1) * rows, rows), 3 * rows), :]
    out_ref[...] = apply_band(hi, lo, window)


def smooth_edge_kernel(last, win_ref, nb_ref, w_ref, out_ref):
    rows = out_ref.shape[0]
    i = pl.program_id(0) * last
    hi, lo = band_of(nb_ref, w_ref, i * rows, rows)
    out_ref[...] = apply_band(hi, lo, win_ref[0])


def smooth_inner(emb, nb_t, w_t, rows):
    seg_rows, rank = emb.shape
    inner = seg_rows // rows - 2
    return pl.pallas_call(
        smooth_inner_kernel,
        grid=(inner,),
        in_specs=[
            pl.BlockSpec(emb.shape, lambda i: (0, 0), pipeline_mode=pl.Buffered(1)),
            pl.BlockSpec((nb_t.shape[0], rows), lambda i: (0, i + 1)),
            pl.BlockSpec((w_t.shape[0], rows), lambda i: (0, i + 1)),
        ],
        out_specs=pl.BlockSpec((rows, rank), lambda i: (i, 0)),
        out_shape=jax.ShapeDtypeStruct((inner * rows, rank), F32),
        compiler_params=pltpu.CompilerParams(dimension_semantics=("arbitrary",)),
    )(emb, nb_t, w_t)


def smooth_edge(windows, nb_t, w_t, rows):
    rank = windows.shape[2]
    last = nb_t.shape[1] // rows - 1
    return pl.pallas_call(
        functools.partial(smooth_edge_kernel, last),
        grid=(2,),
        in_specs=[
            pl.BlockSpec((1,) + windows.shape[1:], lambda i: (i, 0, 0)),
            pl.BlockSpec((nb_t.shape[0], rows), lambda i: (0, i * last)),
            pl.BlockSpec((w_t.shape[0], rows), lambda i: (0, i * last)),
        ],
        out_specs=pl.BlockSpec((rows, rank), lambda i: (i, 0)),
        out_shape=jax.ShapeDtypeStruct((2 * rows, rank), F32),
        compiler_params=pltpu.CompilerParams(dimension_semantics=("arbitrary",)),
    )(windows, nb_t, w_t)


def owned_kernel(tgt_ref, ret_ref, _, out_ref, acc_ref):
    c = pl.program_id(0)
    chunk = ret_ref.shape[0]

    @pl.when(c == 0)
    def _():
        acc_ref[...] = jnp.zeros_like(acc_ref)

    for s in range(chunk):
        b = tgt_ref[c * chunk + s]

        @pl.when(b >= 0)
        def _():
            acc_ref[b] += ret_ref[s].astype(F32)

    @pl.when(c == pl.num_programs(0) - 1)
    def _():
        for b in range(acc_ref.shape[0]):
            out_ref[b] = acc_ref[b].T


def owned_pass(targets, returned, after, block_count, chunk=32):
    slots, rank, block = returned.shape
    return pl.pallas_call(
        owned_kernel,
        grid_spec=pltpu.PrefetchScalarGridSpec(
            num_scalar_prefetch=1,
            grid=(slots // chunk,),
            in_specs=[
                pl.BlockSpec((chunk, rank, block), lambda c, tg: (c, 0, 0)),
                pl.BlockSpec(memory_space=pl.ANY),
            ],
            out_specs=pl.BlockSpec(
                (block_count, block, rank), lambda c, tg: (0, 0, 0), pipeline_mode=pl.Buffered(1)
            ),
            scratch_shapes=[pltpu.VMEM((block_count, rank, block), F32)],
        ),
        out_shape=jax.ShapeDtypeStruct((block_count, block, rank), F32),
        compiler_params=pltpu.CompilerParams(dimension_semantics=("arbitrary",)),
    )(targets, returned, after)


def local(
    emb, lengths, pair_block, feats, proj, targets, trip_weight, send_list, nb_index, nb_weight
):
    block_size = lengths.shape[2]
    rank_width = emb.shape[1]
    seg_rows = emb.shape[0]
    block_count = seg_rows // block_size
    regions = lax.axis_size("region")
    blocks = emb.reshape(block_count, block_size, rank_width)
    send_rows = send_list[0, 0]
    live_mask = send_rows >= 0
    slot_count = send_rows.shape[1]
    outgoing = blocks[jnp.where(live_mask, send_rows, 0)]
    incoming = lax.all_to_all(outgoing, "region", split_axis=0, concat_axis=0, tiled=True)
    incoming = incoming.reshape(regions * slot_count, block_size, rank_width)
    trip_blocks = lengths.shape[0]
    query_t = jnp.einsum("fr,ft->rt", proj, feats, preferred_element_type=F32)

    nb_t = nb_index[0]
    w_t = nb_weight[0]
    inner = smooth_inner(emb, nb_t, w_t, block_size)
    count = regions
    head = emb[:block_size]
    tail = emb[seg_rows - block_size :]
    prev_tail = lax.ppermute(tail, "region", [(i, (i + 1) % count) for i in range(count)])
    next_head = lax.ppermute(head, "region", [((i + 1) % count, i) for i in range(count)])
    windows = jnp.stack(
        [
            jnp.concatenate([prev_tail, emb[: 2 * block_size]], axis=0),
            jnp.concatenate([emb[seg_rows - 2 * block_size :], next_head], axis=0),
        ]
    )
    edge = smooth_edge(windows, nb_t, w_t, block_size)

    pred_rows, slot_grad = trip_pass(
        pair_block.reshape(-1),
        lengths,
        incoming,
        query_t,
        targets.reshape(trip_blocks, 1, block_size),
        trip_weight.reshape(trip_blocks, 1, block_size),
        inner,
    )
    predicted = pred_rows.reshape(trip_blocks * block_size)

    returned = lax.all_to_all(
        slot_grad.reshape(regions, slot_count, rank_width, block_size),
        "region",
        split_axis=0,
        concat_axis=0,
        tiled=True,
    )
    returned = returned.reshape(regions * slot_count, rank_width, block_size)

    target_rows = jnp.where(live_mask, send_rows, -1).reshape(-1)
    owned = owned_pass(target_rows, returned, edge, block_count).reshape(seg_rows, rank_width)
    partner = lax.ppermute(owned, "rep", [(0, 1), (1, 0)])
    smoothed = jnp.concatenate([edge[:block_size], inner, edge[block_size:]], axis=0)
    gradient = (owned + partner) + LAM * smoothed
    return (predicted, gradient.astype(jnp.bfloat16))


def solution(mesh):
    placed = (
        P("region", None),
        P(("region", "rep"), None, None, None),
        P(("region", "rep"), None),
        P(None, ("region", "rep")),
        P(),
        P(("region", "rep")),
        P(("region", "rep")),
        P("region", "rep", None, None),
        P("region", None, None),
        P("region", None, None),
    )
    return jax.shard_map(
        local,
        mesh=mesh,
        in_specs=placed,
        out_specs=(P(("region", "rep")), P("region", None)),
        check_vma=False,
    )
```

```python
import functools

import jax
import jax.numpy as jnp
from jax import lax
from jax.experimental import pallas as pl
from jax.experimental.pallas import tpu as pltpu
from jax.sharding import PartitionSpec as P

LAM = 0.25
F32 = jnp.float32
BF16 = jnp.bfloat16
TN = (((0,), (0,)), ((), ()))


def trip_kernel(
    pair_count, pb_ref, len_ref, inc_ref, qt_ref, tgt_ref, w_ref, _, pred_ref, out_ref, acc_ref
):
    t = pl.program_id(0)

    @pl.when(t == 0)
    def _():
        acc_ref[...] = jnp.zeros_like(acc_ref)

    hidden = None
    for k in range(0, pair_count, 2):
        p0 = pb_ref[t * pair_count + k]
        p1 = pb_ref[t * pair_count + k + 1]
        lhs = jnp.concatenate([len_ref[0, k], len_ref[0, k + 1]], axis=1)
        rhs = jnp.concatenate([inc_ref[p0], inc_ref[p1]], axis=0)
        term = jnp.dot(lhs, rhs, preferred_element_type=F32)
        hidden = term if hidden is None else hidden + term
    q_t = qt_ref[...]
    pred_row = jnp.sum(hidden.T * q_t, axis=0, keepdims=True)
    pred_ref[0] = pred_row
    err_row = w_ref[0] * (pred_row - tgt_ref[0])
    scaled_t = (err_row * q_t).astype(BF16)
    block = q_t.shape[1]
    for k in range(0, pair_count, 2):
        p0 = pb_ref[t * pair_count + k]
        p1 = pb_ref[t * pair_count + k + 1]
        rhs = jnp.concatenate([len_ref[0, k], len_ref[0, k + 1]], axis=1)
        both = jnp.dot(scaled_t, rhs, preferred_element_type=F32)
        acc_ref[p0] += both[:, :block]
        acc_ref[p1] += both[:, block:]

    @pl.when(t == pl.num_programs(0) - 1)
    def _():
        out_ref[...] = acc_ref[...].astype(out_ref.dtype)


def trip_pass(pair_flat, lengths, incoming, query_t, tgt, wts, after):
    trip_blocks, pair_count, block, rank = lengths.shape
    slots = incoming.shape[0]
    const3 = lambda t, pb: (0, 0, 0)
    return pl.pallas_call(
        functools.partial(trip_kernel, pair_count),
        grid_spec=pltpu.PrefetchScalarGridSpec(
            num_scalar_prefetch=1,
            grid=(trip_blocks,),
            in_specs=[
                pl.BlockSpec((1, pair_count, block, block), lambda t, pb: (t, 0, 0, 0)),
                pl.BlockSpec((slots, block, rank), const3, pipeline_mode=pl.Buffered(1)),
                pl.BlockSpec((rank, block), lambda t, pb: (0, t)),
                pl.BlockSpec((1, 1, block), lambda t, pb: (t, 0, 0)),
                pl.BlockSpec((1, 1, block), lambda t, pb: (t, 0, 0)),
                pl.BlockSpec(memory_space=pl.ANY),
            ],
            out_specs=[
                pl.BlockSpec((1, 1, block), lambda t, pb: (t, 0, 0)),
                pl.BlockSpec((slots, block, rank), const3, pipeline_mode=pl.Buffered(1)),
            ],
            scratch_shapes=[pltpu.VMEM((slots, block, rank), F32)],
        ),
        out_shape=[
            jax.ShapeDtypeStruct((trip_blocks, 1, block), F32),
            jax.ShapeDtypeStruct((slots, block, rank), BF16),
        ],
        compiler_params=pltpu.CompilerParams(
            dimension_semantics=("arbitrary",), vmem_limit_bytes=60 * 1024 * 1024
        ),
    )(pair_flat, lengths, incoming, query_t, tgt, wts, after)


def band_of(nb_ref, w_ref, base, rows):
    span = 3 * rows
    row = lax.broadcasted_iota(jnp.int32, (span, rows), 0)
    band = jnp.zeros((span, rows), F32)
    for k in range(nb_ref.shape[0]):
        rel = nb_ref[k : k + 1, :] - base
        band = band - jnp.where(row == rel, w_ref[k : k + 1, :], 0.0)
    mid_row = lax.broadcasted_iota(jnp.int32, (rows, rows), 0)
    mid_col = lax.broadcasted_iota(jnp.int32, (rows, rows), 1)
    total = jnp.sum(w_ref[...], axis=0, keepdims=True)
    mid = band[rows : 2 * rows] + jnp.where(mid_row == mid_col, total, 0.0)
    band = jnp.concatenate([band[:rows], mid, band[2 * rows :]], axis=0)
    hi = band.astype(BF16)
    lo = (band - hi.astype(F32)).astype(BF16)
    return hi, lo


def apply_band(hi, lo, window):
    return lax.dot_general(hi, window, TN, preferred_element_type=F32) + lax.dot_general(
        lo, window, TN, preferred_element_type=F32
    )


def smooth_inner_kernel(emb_ref, nb_ref, w_ref, out_ref):
    rows = out_ref.shape[0]
    i = pl.program_id(0) + 1
    hi, lo = band_of(nb_ref, w_ref, i * rows, rows)
    window = emb_ref[pl.ds(pl.multiple_of((i - 1) * rows, rows), 3 * rows), :]
    out_ref[...] = apply_band(hi, lo, window)


def smooth_edge_kernel(last, win_ref, nb_ref, w_ref, out_ref):
    rows = out_ref.shape[0]
    i = pl.program_id(0) * last
    hi, lo = band_of(nb_ref, w_ref, i * rows, rows)
    out_ref[...] = apply_band(hi, lo, win_ref[0])


def smooth_inner(emb, nb_t, w_t, rows):
    seg_rows, rank = emb.shape
    inner = seg_rows // rows - 2
    return pl.pallas_call(
        smooth_inner_kernel,
        grid=(inner,),
        in_specs=[
            pl.BlockSpec(emb.shape, lambda i: (0, 0), pipeline_mode=pl.Buffered(1)),
            pl.BlockSpec((nb_t.shape[0], rows), lambda i: (0, i + 1)),
            pl.BlockSpec((w_t.shape[0], rows), lambda i: (0, i + 1)),
        ],
        out_specs=pl.BlockSpec((rows, rank), lambda i: (i, 0)),
        out_shape=jax.ShapeDtypeStruct((inner * rows, rank), F32),
        compiler_params=pltpu.CompilerParams(dimension_semantics=("arbitrary",)),
    )(emb, nb_t, w_t)


def smooth_edge(windows, nb_t, w_t, rows):
    rank = windows.shape[2]
    last = nb_t.shape[1] // rows - 1
    return pl.pallas_call(
        functools.partial(smooth_edge_kernel, last),
        grid=(2,),
        in_specs=[
            pl.BlockSpec((1,) + windows.shape[1:], lambda i: (i, 0, 0)),
            pl.BlockSpec((nb_t.shape[0], rows), lambda i: (0, i * last)),
            pl.BlockSpec((w_t.shape[0], rows), lambda i: (0, i * last)),
        ],
        out_specs=pl.BlockSpec((rows, rank), lambda i: (i, 0)),
        out_shape=jax.ShapeDtypeStruct((2 * rows, rank), F32),
        compiler_params=pltpu.CompilerParams(dimension_semantics=("arbitrary",)),
    )(windows, nb_t, w_t)


def owned_kernel(tgt_ref, ret_ref, _, out_ref, acc_ref):
    c = pl.program_id(0)
    chunk = ret_ref.shape[0]

    @pl.when(c == 0)
    def _():
        acc_ref[...] = jnp.zeros_like(acc_ref)

    for s in range(chunk):
        b = tgt_ref[c * chunk + s]

        @pl.when(b >= 0)
        def _():
            acc_ref[b] += ret_ref[s].astype(F32)

    @pl.when(c == pl.num_programs(0) - 1)
    def _():
        for b in range(acc_ref.shape[0]):
            out_ref[b] = acc_ref[b].T


def owned_pass(targets, returned, after, block_count, chunk=32):
    slots, rank, block = returned.shape
    return pl.pallas_call(
        owned_kernel,
        grid_spec=pltpu.PrefetchScalarGridSpec(
            num_scalar_prefetch=1,
            grid=(slots // chunk,),
            in_specs=[
                pl.BlockSpec((chunk, rank, block), lambda c, tg: (c, 0, 0)),
                pl.BlockSpec(memory_space=pl.ANY),
            ],
            out_specs=pl.BlockSpec(
                (block_count, block, rank), lambda c, tg: (0, 0, 0), pipeline_mode=pl.Buffered(1)
            ),
            scratch_shapes=[pltpu.VMEM((block_count, rank, block), F32)],
        ),
        out_shape=jax.ShapeDtypeStruct((block_count, block, rank), F32),
        compiler_params=pltpu.CompilerParams(dimension_semantics=("arbitrary",)),
    )(targets, returned, after)


def gather_kernel(idx_ref, src_ref, out_ref, sems):
    count = out_ref.shape[0]

    def start(s, carry):
        pltpu.make_async_copy(src_ref.at[idx_ref[s]], out_ref.at[s], sems.at[s]).start()
        return carry

    def wait(s, carry):
        pltpu.make_async_copy(src_ref.at[0], out_ref.at[s], sems.at[s]).wait()
        return carry

    lax.fori_loop(0, count, start, 0)
    lax.fori_loop(0, count, wait, 0)


def gather_blocks(idx, blocks):
    count = idx.shape[0]
    return pl.pallas_call(
        gather_kernel,
        grid_spec=pltpu.PrefetchScalarGridSpec(
            num_scalar_prefetch=1,
            grid=(1,),
            in_specs=[pl.BlockSpec(memory_space=pl.ANY)],
            out_specs=pl.BlockSpec(memory_space=pl.ANY),
            scratch_shapes=[pltpu.SemaphoreType.DMA((count,))],
        ),
        out_shape=jax.ShapeDtypeStruct((count,) + blocks.shape[1:], blocks.dtype),
    )(idx, blocks)


def local(
    emb, lengths, pair_block, feats, proj, targets, trip_weight, send_list, nb_index, nb_weight
):
    block_size = lengths.shape[2]
    rank_width = emb.shape[1]
    seg_rows = emb.shape[0]
    block_count = seg_rows // block_size
    regions = lax.axis_size("region")
    blocks = emb.reshape(block_count, block_size, rank_width)
    send_rows = send_list[0, 0]
    live_mask = send_rows >= 0
    slot_count = send_rows.shape[1]
    outgoing = gather_blocks(jnp.where(live_mask, send_rows, 0).reshape(-1), blocks)
    outgoing = outgoing.reshape(regions, slot_count, block_size, rank_width)
    incoming = lax.all_to_all(outgoing, "region", split_axis=0, concat_axis=0, tiled=True)
    incoming = incoming.reshape(regions * slot_count, block_size, rank_width)
    trip_blocks = lengths.shape[0]
    query_t = jnp.einsum("fr,ft->rt", proj, feats, preferred_element_type=F32)

    nb_t = nb_index[0]
    w_t = nb_weight[0]
    inner = smooth_inner(emb, nb_t, w_t, block_size)
    count = regions
    head = emb[:block_size]
    tail = emb[seg_rows - block_size :]
    prev_tail = lax.ppermute(tail, "region", [(i, (i + 1) % count) for i in range(count)])
    next_head = lax.ppermute(head, "region", [((i + 1) % count, i) for i in range(count)])
    windows = jnp.stack(
        [
            jnp.concatenate([prev_tail, emb[: 2 * block_size]], axis=0),
            jnp.concatenate([emb[seg_rows - 2 * block_size :], next_head], axis=0),
        ]
    )
    edge = smooth_edge(windows, nb_t, w_t, block_size)

    pred_rows, slot_grad = trip_pass(
        pair_block.reshape(-1),
        lengths,
        incoming,
        query_t,
        targets.reshape(trip_blocks, 1, block_size),
        trip_weight.reshape(trip_blocks, 1, block_size),
        inner,
    )
    predicted = pred_rows.reshape(trip_blocks * block_size)

    returned = lax.all_to_all(
        slot_grad.reshape(regions, slot_count, rank_width, block_size),
        "region",
        split_axis=0,
        concat_axis=0,
        tiled=True,
    )
    returned = returned.reshape(regions * slot_count, rank_width, block_size)

    target_rows = jnp.where(live_mask, send_rows, -1).reshape(-1)
    owned = owned_pass(target_rows, returned, edge, block_count).reshape(seg_rows, rank_width)
    partner = lax.ppermute(owned, "rep", [(0, 1), (1, 0)])
    smoothed = jnp.concatenate([edge[:block_size], inner, edge[block_size:]], axis=0)
    gradient = (owned + partner) + LAM * smoothed
    return (predicted, gradient.astype(jnp.bfloat16))


def solution(mesh):
    placed = (
        P("region", None),
        P(("region", "rep"), None, None, None),
        P(("region", "rep"), None),
        P(None, ("region", "rep")),
        P(),
        P(("region", "rep")),
        P(("region", "rep")),
        P("region", "rep", None, None),
        P("region", None, None),
        P("region", None, None),
    )
    return jax.shard_map(
        local,
        mesh=mesh,
        in_specs=placed,
        out_specs=(P(("region", "rep")), P("region", None)),
        check_vma=False,
    )
```

```python
import functools

import jax
import jax.numpy as jnp
from jax import lax
from jax.experimental import pallas as pl
from jax.experimental.pallas import tpu as pltpu
from jax.sharding import PartitionSpec as P

LAM = 0.25
F32 = jnp.float32
BF16 = jnp.bfloat16
TN = (((0,), (0,)), ((), ()))


def trip_kernel(
    pair_count, pb_ref, len_ref, inc_ref, qt_ref, tgt_ref, w_ref, _, pred_ref, out_ref, acc_ref
):
    step = pl.program_id(0)
    per_step = len_ref.shape[0]
    block = qt_ref.shape[0]

    @pl.when(step == 0)
    def _():
        acc_ref[...] = jnp.zeros_like(acc_ref)

    for u in range(per_step):
        t = step * per_step + u
        hidden = None
        for k in range(0, pair_count, 2):
            p0 = pb_ref[t * pair_count + k]
            p1 = pb_ref[t * pair_count + k + 1]
            lhs = jnp.concatenate([len_ref[u, k], len_ref[u, k + 1]], axis=1)
            rhs = jnp.concatenate([inc_ref[p0], inc_ref[p1]], axis=0)
            term = jnp.dot(lhs, rhs, preferred_element_type=F32)
            hidden = term if hidden is None else hidden + term
        q_t = qt_ref[:, u * block : (u + 1) * block]
        pred_row = jnp.sum(hidden.T * q_t, axis=0, keepdims=True)
        pred_ref[u] = pred_row
        err_row = w_ref[u] * (pred_row - tgt_ref[u])
        scaled_t = (err_row * q_t).astype(BF16)
        for k in range(0, pair_count, 2):
            p0 = pb_ref[t * pair_count + k]
            p1 = pb_ref[t * pair_count + k + 1]
            rhs = jnp.concatenate([len_ref[u, k], len_ref[u, k + 1]], axis=1)
            both = jnp.dot(scaled_t, rhs, preferred_element_type=F32)
            acc_ref[p0] += both[:, :block]
            acc_ref[p1] += both[:, block:]

    @pl.when(step == pl.num_programs(0) - 1)
    def _():
        out_ref[...] = acc_ref[...].astype(out_ref.dtype)


def trip_pass(pair_flat, lengths, incoming, query_t, tgt, wts, after, per_step=2):
    trip_blocks, pair_count, block, rank = lengths.shape
    slots = incoming.shape[0]
    const3 = lambda t, pb: (0, 0, 0)
    return pl.pallas_call(
        functools.partial(trip_kernel, pair_count),
        grid_spec=pltpu.PrefetchScalarGridSpec(
            num_scalar_prefetch=1,
            grid=(trip_blocks // per_step,),
            in_specs=[
                pl.BlockSpec((per_step, pair_count, block, block), lambda t, pb: (t, 0, 0, 0)),
                pl.BlockSpec((slots, block, rank), const3, pipeline_mode=pl.Buffered(1)),
                pl.BlockSpec((rank, per_step * block), lambda t, pb: (0, t)),
                pl.BlockSpec((per_step, 1, block), lambda t, pb: (t, 0, 0)),
                pl.BlockSpec((per_step, 1, block), lambda t, pb: (t, 0, 0)),
                pl.BlockSpec(memory_space=pl.ANY),
            ],
            out_specs=[
                pl.BlockSpec((per_step, 1, block), lambda t, pb: (t, 0, 0)),
                pl.BlockSpec((slots, block, rank), const3, pipeline_mode=pl.Buffered(1)),
            ],
            scratch_shapes=[pltpu.VMEM((slots, block, rank), F32)],
        ),
        out_shape=[
            jax.ShapeDtypeStruct((trip_blocks, 1, block), F32),
            jax.ShapeDtypeStruct((slots, block, rank), BF16),
        ],
        compiler_params=pltpu.CompilerParams(
            dimension_semantics=("arbitrary",), vmem_limit_bytes=60 * 1024 * 1024
        ),
    )(pair_flat, lengths, incoming, query_t, tgt, wts, after)


def band_of(nb_ref, w_ref, base, rows):
    span = 3 * rows
    row = lax.broadcasted_iota(jnp.int32, (span, rows), 0)
    band = jnp.zeros((span, rows), F32)
    for k in range(nb_ref.shape[0]):
        rel = nb_ref[k : k + 1, :] - base
        band = band - jnp.where(row == rel, w_ref[k : k + 1, :], 0.0)
    mid_row = lax.broadcasted_iota(jnp.int32, (rows, rows), 0)
    mid_col = lax.broadcasted_iota(jnp.int32, (rows, rows), 1)
    total = jnp.sum(w_ref[...], axis=0, keepdims=True)
    mid = band[rows : 2 * rows] + jnp.where(mid_row == mid_col, total, 0.0)
    band = jnp.concatenate([band[:rows], mid, band[2 * rows :]], axis=0)
    hi = band.astype(BF16)
    lo = (band - hi.astype(F32)).astype(BF16)
    return hi, lo


def apply_band(hi, lo, window):
    return lax.dot_general(hi, window, TN, preferred_element_type=F32) + lax.dot_general(
        lo, window, TN, preferred_element_type=F32
    )


def smooth_inner_kernel(emb_ref, nb_ref, w_ref, out_ref):
    rows = out_ref.shape[0]
    i = pl.program_id(0) + 1
    hi, lo = band_of(nb_ref, w_ref, i * rows, rows)
    window = emb_ref[pl.ds(pl.multiple_of((i - 1) * rows, rows), 3 * rows), :]
    out_ref[...] = apply_band(hi, lo, window)


def smooth_edge_kernel(last, win_ref, nb_ref, w_ref, out_ref):
    rows = out_ref.shape[0]
    i = pl.program_id(0) * last
    hi, lo = band_of(nb_ref, w_ref, i * rows, rows)
    out_ref[...] = apply_band(hi, lo, win_ref[0])


def smooth_inner(emb, nb_t, w_t, rows):
    seg_rows, rank = emb.shape
    inner = seg_rows // rows - 2
    return pl.pallas_call(
        smooth_inner_kernel,
        grid=(inner,),
        in_specs=[
            pl.BlockSpec(emb.shape, lambda i: (0, 0), pipeline_mode=pl.Buffered(1)),
            pl.BlockSpec((nb_t.shape[0], rows), lambda i: (0, i + 1)),
            pl.BlockSpec((w_t.shape[0], rows), lambda i: (0, i + 1)),
        ],
        out_specs=pl.BlockSpec((rows, rank), lambda i: (i, 0)),
        out_shape=jax.ShapeDtypeStruct((inner * rows, rank), F32),
        compiler_params=pltpu.CompilerParams(dimension_semantics=("arbitrary",)),
    )(emb, nb_t, w_t)


def smooth_edge(windows, nb_t, w_t, rows):
    rank = windows.shape[2]
    last = nb_t.shape[1] // rows - 1
    return pl.pallas_call(
        functools.partial(smooth_edge_kernel, last),
        grid=(2,),
        in_specs=[
            pl.BlockSpec((1,) + windows.shape[1:], lambda i: (i, 0, 0)),
            pl.BlockSpec((nb_t.shape[0], rows), lambda i: (0, i * last)),
            pl.BlockSpec((w_t.shape[0], rows), lambda i: (0, i * last)),
        ],
        out_specs=pl.BlockSpec((rows, rank), lambda i: (i, 0)),
        out_shape=jax.ShapeDtypeStruct((2 * rows, rank), F32),
        compiler_params=pltpu.CompilerParams(dimension_semantics=("arbitrary",)),
    )(windows, nb_t, w_t)


def owned_kernel(tgt_ref, ret_ref, _, out_ref, acc_ref):
    c = pl.program_id(0)
    chunk = ret_ref.shape[0]

    @pl.when(c == 0)
    def _():
        acc_ref[...] = jnp.zeros_like(acc_ref)

    for s in range(chunk):
        b = tgt_ref[c * chunk + s]

        @pl.when(b >= 0)
        def _():
            acc_ref[b] += ret_ref[s].astype(F32)

    @pl.when(c == pl.num_programs(0) - 1)
    def _():
        for b in range(acc_ref.shape[0]):
            out_ref[b] = acc_ref[b].T


def owned_pass(targets, returned, after, block_count, chunk=32):
    slots, rank, block = returned.shape
    return pl.pallas_call(
        owned_kernel,
        grid_spec=pltpu.PrefetchScalarGridSpec(
            num_scalar_prefetch=1,
            grid=(slots // chunk,),
            in_specs=[
                pl.BlockSpec((chunk, rank, block), lambda c, tg: (c, 0, 0)),
                pl.BlockSpec(memory_space=pl.ANY),
            ],
            out_specs=pl.BlockSpec(
                (block_count, block, rank), lambda c, tg: (0, 0, 0), pipeline_mode=pl.Buffered(1)
            ),
            scratch_shapes=[pltpu.VMEM((block_count, rank, block), F32)],
        ),
        out_shape=jax.ShapeDtypeStruct((block_count, block, rank), F32),
        compiler_params=pltpu.CompilerParams(dimension_semantics=("arbitrary",)),
    )(targets, returned, after)


def gather_kernel(idx_ref, src_ref, out_ref):
    c = pl.program_id(0)
    chunk = out_ref.shape[0]
    for s in range(chunk):
        out_ref[s] = src_ref[idx_ref[c * chunk + s]]


def gather_blocks(idx, blocks, chunk=32):
    count = idx.shape[0]
    return pl.pallas_call(
        gather_kernel,
        grid_spec=pltpu.PrefetchScalarGridSpec(
            num_scalar_prefetch=1,
            grid=(count // chunk,),
            in_specs=[
                pl.BlockSpec(blocks.shape, lambda c, ix: (0, 0, 0), pipeline_mode=pl.Buffered(1))
            ],
            out_specs=pl.BlockSpec((chunk,) + blocks.shape[1:], lambda c, ix: (c, 0, 0)),
        ),
        out_shape=jax.ShapeDtypeStruct((count,) + blocks.shape[1:], blocks.dtype),
    )(idx, blocks)


def local(
    emb, lengths, pair_block, feats, proj, targets, trip_weight, send_list, nb_index, nb_weight
):
    block_size = lengths.shape[2]
    rank_width = emb.shape[1]
    seg_rows = emb.shape[0]
    block_count = seg_rows // block_size
    regions = lax.axis_size("region")
    blocks = emb.reshape(block_count, block_size, rank_width)
    send_rows = send_list[0, 0]
    live_mask = send_rows >= 0
    slot_count = send_rows.shape[1]
    outgoing = gather_blocks(jnp.where(live_mask, send_rows, 0).reshape(-1), blocks)
    outgoing = outgoing.reshape(regions, slot_count, block_size, rank_width)
    incoming = lax.all_to_all(outgoing, "region", split_axis=0, concat_axis=0, tiled=True)
    incoming = incoming.reshape(regions * slot_count, block_size, rank_width)
    trip_blocks = lengths.shape[0]
    query_t = jnp.einsum("fr,ft->rt", proj, feats, preferred_element_type=F32)

    nb_t = nb_index[0]
    w_t = nb_weight[0]
    inner = smooth_inner(emb, nb_t, w_t, block_size)
    count = regions
    head = emb[:block_size]
    tail = emb[seg_rows - block_size :]
    prev_tail = lax.ppermute(tail, "region", [(i, (i + 1) % count) for i in range(count)])
    next_head = lax.ppermute(head, "region", [((i + 1) % count, i) for i in range(count)])
    windows = jnp.stack(
        [
            jnp.concatenate([prev_tail, emb[: 2 * block_size]], axis=0),
            jnp.concatenate([emb[seg_rows - 2 * block_size :], next_head], axis=0),
        ]
    )
    edge = smooth_edge(windows, nb_t, w_t, block_size)

    pred_rows, slot_grad = trip_pass(
        pair_block.reshape(-1),
        lengths,
        incoming,
        query_t,
        targets.reshape(trip_blocks, 1, block_size),
        trip_weight.reshape(trip_blocks, 1, block_size),
        inner,
    )
    predicted = pred_rows.reshape(trip_blocks * block_size)

    returned = lax.all_to_all(
        slot_grad.reshape(regions, slot_count, rank_width, block_size),
        "region",
        split_axis=0,
        concat_axis=0,
        tiled=True,
    )
    returned = returned.reshape(regions * slot_count, rank_width, block_size)

    target_rows = jnp.where(live_mask, send_rows, -1).reshape(-1)
    owned = owned_pass(target_rows, returned, edge, block_count).reshape(seg_rows, rank_width)
    partner = lax.ppermute(owned, "rep", [(0, 1), (1, 0)])
    smoothed = jnp.concatenate([edge[:block_size], inner, edge[block_size:]], axis=0)
    gradient = (owned + partner) + LAM * smoothed
    return (predicted, gradient.astype(jnp.bfloat16))


def solution(mesh):
    placed = (
        P("region", None),
        P(("region", "rep"), None, None, None),
        P(("region", "rep"), None),
        P(None, ("region", "rep")),
        P(),
        P(("region", "rep")),
        P(("region", "rep")),
        P("region", "rep", None, None),
        P("region", None, None),
        P("region", None, None),
    )
    return jax.shard_map(
        local,
        mesh=mesh,
        in_specs=placed,
        out_specs=(P(("region", "rep")), P("region", None)),
        check_vma=False,
    )
```

```python
import functools

import jax
import jax.numpy as jnp
from jax import lax
from jax.experimental import pallas as pl
from jax.experimental.pallas import tpu as pltpu
from jax.sharding import PartitionSpec as P

LAM = 0.25
F32 = jnp.float32
BF16 = jnp.bfloat16
TN = (((0,), (0,)), ((), ()))


def trip_kernel(
    pair_count, pb_ref, len_ref, inc_ref, qt_ref, tgt_ref, w_ref, _, pred_ref, out_ref, acc_ref
):
    step = pl.program_id(0)
    per_step = len_ref.shape[0]
    block = qt_ref.shape[0]

    @pl.when(step == 0)
    def _():
        acc_ref[...] = jnp.zeros_like(acc_ref)

    for u in range(per_step):
        t = step * per_step + u
        hidden = None
        for k in range(0, pair_count, 2):
            p0 = pb_ref[t * pair_count + k]
            p1 = pb_ref[t * pair_count + k + 1]
            lhs = jnp.concatenate([len_ref[u, k], len_ref[u, k + 1]], axis=1)
            rhs = jnp.concatenate([inc_ref[p0], inc_ref[p1]], axis=0)
            term = jnp.dot(lhs, rhs, preferred_element_type=F32)
            hidden = term if hidden is None else hidden + term
        q_t = qt_ref[:, u * block : (u + 1) * block]
        pred_row = jnp.sum(hidden.T * q_t, axis=0, keepdims=True)
        pred_ref[u] = pred_row
        err_row = w_ref[u] * (pred_row - tgt_ref[u])
        scaled_t = (err_row * q_t).astype(BF16)
        for k in range(0, pair_count, 2):
            p0 = pb_ref[t * pair_count + k]
            p1 = pb_ref[t * pair_count + k + 1]
            rhs = jnp.concatenate([len_ref[u, k], len_ref[u, k + 1]], axis=1)
            both = jnp.dot(scaled_t, rhs, preferred_element_type=F32)
            acc_ref[p0] += both[:, :block]
            acc_ref[p1] += both[:, block:]

    @pl.when(step == pl.num_programs(0) - 1)
    def _():
        out_ref[...] = acc_ref[...].astype(out_ref.dtype)


def trip_pass(pair_flat, lengths, incoming, query_t, tgt, wts, after, per_step=4):
    trip_blocks, pair_count, block, rank = lengths.shape
    slots = incoming.shape[0]
    const3 = lambda t, pb: (0, 0, 0)
    return pl.pallas_call(
        functools.partial(trip_kernel, pair_count),
        grid_spec=pltpu.PrefetchScalarGridSpec(
            num_scalar_prefetch=1,
            grid=(trip_blocks // per_step,),
            in_specs=[
                pl.BlockSpec((per_step, pair_count, block, block), lambda t, pb: (t, 0, 0, 0)),
                pl.BlockSpec((slots, block, rank), const3, pipeline_mode=pl.Buffered(1)),
                pl.BlockSpec((rank, per_step * block), lambda t, pb: (0, t)),
                pl.BlockSpec((per_step, 1, block), lambda t, pb: (t, 0, 0)),
                pl.BlockSpec((per_step, 1, block), lambda t, pb: (t, 0, 0)),
                pl.BlockSpec(memory_space=pl.ANY),
            ],
            out_specs=[
                pl.BlockSpec((per_step, 1, block), lambda t, pb: (t, 0, 0)),
                pl.BlockSpec((slots, block, rank), const3, pipeline_mode=pl.Buffered(1)),
            ],
            scratch_shapes=[pltpu.VMEM((slots, block, rank), F32)],
        ),
        out_shape=[
            jax.ShapeDtypeStruct((trip_blocks, 1, block), F32),
            jax.ShapeDtypeStruct((slots, block, rank), BF16),
        ],
        compiler_params=pltpu.CompilerParams(
            dimension_semantics=("arbitrary",), vmem_limit_bytes=60 * 1024 * 1024
        ),
    )(pair_flat, lengths, incoming, query_t, tgt, wts, after)


def band_of(nb_ref, w_ref, base, rows):
    span = 3 * rows
    row = lax.broadcasted_iota(jnp.int32, (span, rows), 0)
    band = jnp.zeros((span, rows), F32)
    for k in range(nb_ref.shape[0]):
        rel = nb_ref[k : k + 1, :] - base
        band = band - jnp.where(row == rel, w_ref[k : k + 1, :], 0.0)
    mid_row = lax.broadcasted_iota(jnp.int32, (rows, rows), 0)
    mid_col = lax.broadcasted_iota(jnp.int32, (rows, rows), 1)
    total = jnp.sum(w_ref[...], axis=0, keepdims=True)
    mid = band[rows : 2 * rows] + jnp.where(mid_row == mid_col, total, 0.0)
    band = jnp.concatenate([band[:rows], mid, band[2 * rows :]], axis=0)
    hi = band.astype(BF16)
    lo = (band - hi.astype(F32)).astype(BF16)
    return hi, lo


def apply_band(hi, lo, window):
    return lax.dot_general(hi, window, TN, preferred_element_type=F32) + lax.dot_general(
        lo, window, TN, preferred_element_type=F32
    )


def smooth_inner_kernel(emb_ref, nb_ref, w_ref, out_ref):
    rows = out_ref.shape[0]
    i = pl.program_id(0) + 1
    hi, lo = band_of(nb_ref, w_ref, i * rows, rows)
    window = emb_ref[pl.ds(pl.multiple_of((i - 1) * rows, rows), 3 * rows), :]
    out_ref[...] = apply_band(hi, lo, window)


def smooth_edge_kernel(last, win_ref, nb_ref, w_ref, out_ref):
    rows = out_ref.shape[0]
    i = pl.program_id(0) * last
    hi, lo = band_of(nb_ref, w_ref, i * rows, rows)
    out_ref[...] = apply_band(hi, lo, win_ref[0])


def smooth_inner(emb, nb_t, w_t, rows):
    seg_rows, rank = emb.shape
    inner = seg_rows // rows - 2
    return pl.pallas_call(
        smooth_inner_kernel,
        grid=(inner,),
        in_specs=[
            pl.BlockSpec(emb.shape, lambda i: (0, 0), pipeline_mode=pl.Buffered(1)),
            pl.BlockSpec((nb_t.shape[0], rows), lambda i: (0, i + 1)),
            pl.BlockSpec((w_t.shape[0], rows), lambda i: (0, i + 1)),
        ],
        out_specs=pl.BlockSpec((rows, rank), lambda i: (i, 0)),
        out_shape=jax.ShapeDtypeStruct((inner * rows, rank), F32),
        compiler_params=pltpu.CompilerParams(dimension_semantics=("arbitrary",)),
    )(emb, nb_t, w_t)


def smooth_edge(windows, nb_t, w_t, rows):
    rank = windows.shape[2]
    last = nb_t.shape[1] // rows - 1
    return pl.pallas_call(
        functools.partial(smooth_edge_kernel, last),
        grid=(2,),
        in_specs=[
            pl.BlockSpec((1,) + windows.shape[1:], lambda i: (i, 0, 0)),
            pl.BlockSpec((nb_t.shape[0], rows), lambda i: (0, i * last)),
            pl.BlockSpec((w_t.shape[0], rows), lambda i: (0, i * last)),
        ],
        out_specs=pl.BlockSpec((rows, rank), lambda i: (i, 0)),
        out_shape=jax.ShapeDtypeStruct((2 * rows, rank), F32),
        compiler_params=pltpu.CompilerParams(dimension_semantics=("arbitrary",)),
    )(windows, nb_t, w_t)


def owned_kernel(tgt_ref, ret_ref, _, out_ref, acc_ref):
    c = pl.program_id(0)
    chunk = ret_ref.shape[0]

    @pl.when(c == 0)
    def _():
        acc_ref[...] = jnp.zeros_like(acc_ref)

    for s in range(chunk):
        b = tgt_ref[c * chunk + s]

        @pl.when(b >= 0)
        def _():
            acc_ref[b] += ret_ref[s].astype(F32)

    @pl.when(c == pl.num_programs(0) - 1)
    def _():
        for b in range(acc_ref.shape[0]):
            out_ref[b] = acc_ref[b].T


def owned_pass(targets, returned, after, block_count, chunk=32):
    slots, rank, block = returned.shape
    return pl.pallas_call(
        owned_kernel,
        grid_spec=pltpu.PrefetchScalarGridSpec(
            num_scalar_prefetch=1,
            grid=(slots // chunk,),
            in_specs=[
                pl.BlockSpec((chunk, rank, block), lambda c, tg: (c, 0, 0)),
                pl.BlockSpec(memory_space=pl.ANY),
            ],
            out_specs=pl.BlockSpec(
                (block_count, block, rank), lambda c, tg: (0, 0, 0), pipeline_mode=pl.Buffered(1)
            ),
            scratch_shapes=[pltpu.VMEM((block_count, rank, block), F32)],
        ),
        out_shape=jax.ShapeDtypeStruct((block_count, block, rank), F32),
        compiler_params=pltpu.CompilerParams(dimension_semantics=("arbitrary",)),
    )(targets, returned, after)


def gather_kernel(idx_ref, src_ref, out_ref):
    c = pl.program_id(0)
    chunk = out_ref.shape[0]
    for s in range(chunk):
        out_ref[s] = src_ref[idx_ref[c * chunk + s]]


def gather_blocks(idx, blocks, chunk=128):
    count = idx.shape[0]
    return pl.pallas_call(
        gather_kernel,
        grid_spec=pltpu.PrefetchScalarGridSpec(
            num_scalar_prefetch=1,
            grid=(count // chunk,),
            in_specs=[
                pl.BlockSpec(blocks.shape, lambda c, ix: (0, 0, 0), pipeline_mode=pl.Buffered(1))
            ],
            out_specs=pl.BlockSpec((chunk,) + blocks.shape[1:], lambda c, ix: (c, 0, 0)),
        ),
        out_shape=jax.ShapeDtypeStruct((count,) + blocks.shape[1:], blocks.dtype),
    )(idx, blocks)


def local(
    emb, lengths, pair_block, feats, proj, targets, trip_weight, send_list, nb_index, nb_weight
):
    block_size = lengths.shape[2]
    rank_width = emb.shape[1]
    seg_rows = emb.shape[0]
    block_count = seg_rows // block_size
    regions = lax.axis_size("region")
    blocks = emb.reshape(block_count, block_size, rank_width)
    send_rows = send_list[0, 0]
    live_mask = send_rows >= 0
    slot_count = send_rows.shape[1]
    outgoing = gather_blocks(jnp.where(live_mask, send_rows, 0).reshape(-1), blocks)
    outgoing = outgoing.reshape(regions, slot_count, block_size, rank_width)
    incoming = lax.all_to_all(outgoing, "region", split_axis=0, concat_axis=0, tiled=True)
    incoming = incoming.reshape(regions * slot_count, block_size, rank_width)
    trip_blocks = lengths.shape[0]
    query_t = jnp.einsum("fr,ft->rt", proj, feats, preferred_element_type=F32)

    nb_t = nb_index[0]
    w_t = nb_weight[0]
    inner = smooth_inner(emb, nb_t, w_t, block_size)
    count = regions
    head = emb[:block_size]
    tail = emb[seg_rows - block_size :]
    prev_tail = lax.ppermute(tail, "region", [(i, (i + 1) % count) for i in range(count)])
    next_head = lax.ppermute(head, "region", [((i + 1) % count, i) for i in range(count)])
    windows = jnp.stack(
        [
            jnp.concatenate([prev_tail, emb[: 2 * block_size]], axis=0),
            jnp.concatenate([emb[seg_rows - 2 * block_size :], next_head], axis=0),
        ]
    )
    edge = smooth_edge(windows, nb_t, w_t, block_size)

    pred_rows, slot_grad = trip_pass(
        pair_block.reshape(-1),
        lengths,
        incoming,
        query_t,
        targets.reshape(trip_blocks, 1, block_size),
        trip_weight.reshape(trip_blocks, 1, block_size),
        inner,
    )
    predicted = pred_rows.reshape(trip_blocks * block_size)

    returned = lax.all_to_all(
        slot_grad.reshape(regions, slot_count, rank_width, block_size),
        "region",
        split_axis=0,
        concat_axis=0,
        tiled=True,
    )
    returned = returned.reshape(regions * slot_count, rank_width, block_size)

    target_rows = jnp.where(live_mask, send_rows, -1).reshape(-1)
    owned = owned_pass(target_rows, returned, edge, block_count).reshape(seg_rows, rank_width)
    partner = lax.ppermute(owned, "rep", [(0, 1), (1, 0)])
    smoothed = jnp.concatenate([edge[:block_size], inner, edge[block_size:]], axis=0)
    gradient = (owned + partner) + LAM * smoothed
    return (predicted, gradient.astype(jnp.bfloat16))


def solution(mesh):
    placed = (
        P("region", None),
        P(("region", "rep"), None, None, None),
        P(("region", "rep"), None),
        P(None, ("region", "rep")),
        P(),
        P(("region", "rep")),
        P(("region", "rep")),
        P("region", "rep", None, None),
        P("region", None, None),
        P("region", None, None),
    )
    return jax.shard_map(
        local,
        mesh=mesh,
        in_specs=placed,
        out_specs=(P(("region", "rep")), P("region", None)),
        check_vma=False,
    )
```

```python
import functools

import jax
import jax.numpy as jnp
from jax import lax
from jax.experimental import pallas as pl
from jax.experimental.pallas import tpu as pltpu
from jax.sharding import PartitionSpec as P

LAM = 0.25
F32 = jnp.float32
BF16 = jnp.bfloat16
TN = (((0,), (0,)), ((), ()))


def trip_kernel(
    pair_count, trip_steps, pb_ref, len_ref, inc_ref, qt_ref, tgt_ref, w_ref, _, pred_ref, out_ref,
    acc_ref,
):
    step = pl.program_id(0)
    per_step = len_ref.shape[0]
    block = qt_ref.shape[0]

    @pl.when(step == 0)
    def _():
        acc_ref[...] = jnp.zeros_like(acc_ref)

    @pl.when(step < trip_steps)
    def _():
        for u in range(per_step):
            t = step * per_step + u
            hidden = None
            for k in range(0, pair_count, 2):
                p0 = pb_ref[t * pair_count + k]
                p1 = pb_ref[t * pair_count + k + 1]
                lhs = jnp.concatenate([len_ref[u, k], len_ref[u, k + 1]], axis=1)
                rhs = jnp.concatenate([inc_ref[p0], inc_ref[p1]], axis=0)
                term = jnp.dot(lhs, rhs, preferred_element_type=F32)
                hidden = term if hidden is None else hidden + term
            q_t = qt_ref[:, u * block : (u + 1) * block]
            pred_row = jnp.sum(hidden.T * q_t, axis=0, keepdims=True)
            pred_ref[u] = pred_row
            err_row = w_ref[u] * (pred_row - tgt_ref[u])
            scaled_t = (err_row * q_t).astype(BF16)
            for k in range(0, pair_count, 2):
                p0 = pb_ref[t * pair_count + k]
                p1 = pb_ref[t * pair_count + k + 1]
                rhs = jnp.concatenate([len_ref[u, k], len_ref[u, k + 1]], axis=1)
                both = jnp.dot(scaled_t, rhs, preferred_element_type=F32)
                acc_ref[p0] += both[:, :block]
                acc_ref[p1] += both[:, block:]

    @pl.when(step >= trip_steps)
    def _():
        chunk = out_ref.shape[0]
        first = pl.multiple_of((step - trip_steps) * chunk, chunk)
        out_ref[...] = acc_ref[pl.ds(first, chunk)].astype(out_ref.dtype)


def trip_pass(pair_flat, lengths, incoming, query_t, tgt, wts, after, per_step=4, flush=4):
    trip_blocks, pair_count, block, rank = lengths.shape
    slots = incoming.shape[0]
    trip_steps = trip_blocks // per_step
    chunk = slots // flush
    last = trip_steps - 1
    const3 = lambda t, pb: (0, 0, 0)
    return pl.pallas_call(
        functools.partial(trip_kernel, pair_count, trip_steps),
        grid_spec=pltpu.PrefetchScalarGridSpec(
            num_scalar_prefetch=1,
            grid=(trip_steps + flush,),
            in_specs=[
                pl.BlockSpec(
                    (per_step, pair_count, block, block),
                    lambda t, pb: (jnp.minimum(t, last), 0, 0, 0),
                ),
                pl.BlockSpec((slots, block, rank), const3, pipeline_mode=pl.Buffered(1)),
                pl.BlockSpec((rank, per_step * block), lambda t, pb: (0, jnp.minimum(t, last))),
                pl.BlockSpec((per_step, 1, block), lambda t, pb: (jnp.minimum(t, last), 0, 0)),
                pl.BlockSpec((per_step, 1, block), lambda t, pb: (jnp.minimum(t, last), 0, 0)),
                pl.BlockSpec(memory_space=pl.ANY),
            ],
            out_specs=[
                pl.BlockSpec((per_step, 1, block), lambda t, pb: (jnp.minimum(t, last), 0, 0)),
                pl.BlockSpec(
                    (chunk, block, rank), lambda t, pb: (jnp.maximum(t - trip_steps, 0), 0, 0)
                ),
            ],
            scratch_shapes=[pltpu.VMEM((slots, block, rank), F32)],
        ),
        out_shape=[
            jax.ShapeDtypeStruct((trip_blocks, 1, block), F32),
            jax.ShapeDtypeStruct((slots, block, rank), BF16),
        ],
        compiler_params=pltpu.CompilerParams(
            dimension_semantics=("arbitrary",), vmem_limit_bytes=60 * 1024 * 1024
        ),
    )(pair_flat, lengths, incoming, query_t, tgt, wts, after)


def band_of(nb_ref, w_ref, base, rows):
    span = 3 * rows
    row = lax.broadcasted_iota(jnp.int32, (span, rows), 0)
    band = jnp.zeros((span, rows), F32)
    for k in range(nb_ref.shape[0]):
        rel = nb_ref[k : k + 1, :] - base
        band = band - jnp.where(row == rel, w_ref[k : k + 1, :], 0.0)
    mid_row = lax.broadcasted_iota(jnp.int32, (rows, rows), 0)
    mid_col = lax.broadcasted_iota(jnp.int32, (rows, rows), 1)
    total = jnp.sum(w_ref[...], axis=0, keepdims=True)
    mid = band[rows : 2 * rows] + jnp.where(mid_row == mid_col, total, 0.0)
    band = jnp.concatenate([band[:rows], mid, band[2 * rows :]], axis=0)
    hi = band.astype(BF16)
    lo = (band - hi.astype(F32)).astype(BF16)
    return hi, lo


def apply_band(hi, lo, window):
    return lax.dot_general(hi, window, TN, preferred_element_type=F32) + lax.dot_general(
        lo, window, TN, preferred_element_type=F32
    )


def smooth_inner_kernel(emb_ref, nb_ref, w_ref, out_ref):
    rows = out_ref.shape[0]
    i = pl.program_id(0) + 1
    hi, lo = band_of(nb_ref, w_ref, i * rows, rows)
    window = emb_ref[pl.ds(pl.multiple_of((i - 1) * rows, rows), 3 * rows), :]
    out_ref[...] = apply_band(hi, lo, window)


def smooth_edge_kernel(last, win_ref, nb_ref, w_ref, out_ref):
    rows = out_ref.shape[0]
    i = pl.program_id(0) * last
    hi, lo = band_of(nb_ref, w_ref, i * rows, rows)
    out_ref[...] = apply_band(hi, lo, win_ref[0])


def smooth_inner(emb, nb_t, w_t, rows):
    seg_rows, rank = emb.shape
    inner = seg_rows // rows - 2
    return pl.pallas_call(
        smooth_inner_kernel,
        grid=(inner,),
        in_specs=[
            pl.BlockSpec(emb.shape, lambda i: (0, 0), pipeline_mode=pl.Buffered(1)),
            pl.BlockSpec((nb_t.shape[0], rows), lambda i: (0, i + 1)),
            pl.BlockSpec((w_t.shape[0], rows), lambda i: (0, i + 1)),
        ],
        out_specs=pl.BlockSpec((rows, rank), lambda i: (i, 0)),
        out_shape=jax.ShapeDtypeStruct((inner * rows, rank), F32),
        compiler_params=pltpu.CompilerParams(dimension_semantics=("arbitrary",)),
    )(emb, nb_t, w_t)


def smooth_edge(windows, nb_t, w_t, rows):
    rank = windows.shape[2]
    last = nb_t.shape[1] // rows - 1
    return pl.pallas_call(
        functools.partial(smooth_edge_kernel, last),
        grid=(2,),
        in_specs=[
            pl.BlockSpec((1,) + windows.shape[1:], lambda i: (i, 0, 0)),
            pl.BlockSpec((nb_t.shape[0], rows), lambda i: (0, i * last)),
            pl.BlockSpec((w_t.shape[0], rows), lambda i: (0, i * last)),
        ],
        out_specs=pl.BlockSpec((rows, rank), lambda i: (i, 0)),
        out_shape=jax.ShapeDtypeStruct((2 * rows, rank), F32),
        compiler_params=pltpu.CompilerParams(dimension_semantics=("arbitrary",)),
    )(windows, nb_t, w_t)


def owned_kernel(tgt_ref, ret_ref, _, out_ref):
    c = pl.program_id(0)
    chunk = ret_ref.shape[0]

    @pl.when(c == 0)
    def _():
        out_ref[...] = jnp.zeros_like(out_ref)

    for s in range(chunk):
        b = tgt_ref[c * chunk + s]

        @pl.when(b >= 0)
        def _():
            out_ref[b] += ret_ref[s].astype(F32)

    @pl.when(c == pl.num_programs(0) - 1)
    def _():
        for b in range(out_ref.shape[0]):
            out_ref[b] = out_ref[b].T


def owned_pass(targets, returned, after, block_count, chunk=64):
    slots, rank, block = returned.shape
    return pl.pallas_call(
        owned_kernel,
        grid_spec=pltpu.PrefetchScalarGridSpec(
            num_scalar_prefetch=1,
            grid=(slots // chunk,),
            in_specs=[
                pl.BlockSpec((chunk, rank, block), lambda c, tg: (c, 0, 0)),
                pl.BlockSpec(memory_space=pl.ANY),
            ],
            out_specs=pl.BlockSpec(
                (block_count, rank, block), lambda c, tg: (0, 0, 0), pipeline_mode=pl.Buffered(1)
            ),
        ),
        out_shape=jax.ShapeDtypeStruct((block_count, rank, block), F32),
        compiler_params=pltpu.CompilerParams(dimension_semantics=("arbitrary",)),
    )(targets, returned, after)


def gather_kernel(idx_ref, src_ref, out_ref):
    c = pl.program_id(0)
    chunk = out_ref.shape[0]
    for s in range(chunk):
        out_ref[s] = src_ref[idx_ref[c * chunk + s]]


def gather_blocks(idx, blocks, chunk=128):
    count = idx.shape[0]
    return pl.pallas_call(
        gather_kernel,
        grid_spec=pltpu.PrefetchScalarGridSpec(
            num_scalar_prefetch=1,
            grid=(count // chunk,),
            in_specs=[
                pl.BlockSpec(blocks.shape, lambda c, ix: (0, 0, 0), pipeline_mode=pl.Buffered(1))
            ],
            out_specs=pl.BlockSpec((chunk,) + blocks.shape[1:], lambda c, ix: (c, 0, 0)),
        ),
        out_shape=jax.ShapeDtypeStruct((count,) + blocks.shape[1:], blocks.dtype),
    )(idx, blocks)


def local(
    emb, lengths, pair_block, feats, proj, targets, trip_weight, send_list, nb_index, nb_weight
):
    block_size = lengths.shape[2]
    rank_width = emb.shape[1]
    seg_rows = emb.shape[0]
    block_count = seg_rows // block_size
    regions = lax.axis_size("region")
    blocks = emb.reshape(block_count, block_size, rank_width)
    send_rows = send_list[0, 0]
    live_mask = send_rows >= 0
    slot_count = send_rows.shape[1]
    outgoing = gather_blocks(jnp.where(live_mask, send_rows, 0).reshape(-1), blocks)
    outgoing = outgoing.reshape(regions, slot_count, block_size, rank_width)
    incoming = lax.all_to_all(outgoing, "region", split_axis=0, concat_axis=0, tiled=True)
    incoming = incoming.reshape(regions * slot_count, block_size, rank_width)
    trip_blocks = lengths.shape[0]
    query_t = jnp.einsum("fr,ft->rt", proj, feats, preferred_element_type=F32)

    nb_t = nb_index[0]
    w_t = nb_weight[0]
    inner = smooth_inner(emb, nb_t, w_t, block_size)
    count = regions
    head = emb[:block_size]
    tail = emb[seg_rows - block_size :]
    prev_tail = lax.ppermute(tail, "region", [(i, (i + 1) % count) for i in range(count)])
    next_head = lax.ppermute(head, "region", [((i + 1) % count, i) for i in range(count)])
    windows = jnp.stack(
        [
            jnp.concatenate([prev_tail, emb[: 2 * block_size]], axis=0),
            jnp.concatenate([emb[seg_rows - 2 * block_size :], next_head], axis=0),
        ]
    )
    edge = smooth_edge(windows, nb_t, w_t, block_size)

    pred_rows, slot_grad = trip_pass(
        pair_block.reshape(-1),
        lengths,
        incoming,
        query_t,
        targets.reshape(trip_blocks, 1, block_size),
        trip_weight.reshape(trip_blocks, 1, block_size),
        inner,
    )
    predicted = pred_rows.reshape(trip_blocks * block_size)

    returned = lax.all_to_all(
        slot_grad.reshape(regions, slot_count, rank_width, block_size),
        "region",
        split_axis=0,
        concat_axis=0,
        tiled=True,
    )
    returned = returned.reshape(regions * slot_count, rank_width, block_size)

    target_rows = jnp.where(live_mask, send_rows, -1).reshape(-1)
    owned = owned_pass(target_rows, returned, edge, block_count).reshape(seg_rows, rank_width)
    partner = lax.ppermute(owned, "rep", [(0, 1), (1, 0)])
    smoothed = jnp.concatenate([edge[:block_size], inner, edge[block_size:]], axis=0)
    gradient = (owned + partner) + LAM * smoothed
    return (predicted, gradient.astype(jnp.bfloat16))


def solution(mesh):
    placed = (
        P("region", None),
        P(("region", "rep"), None, None, None),
        P(("region", "rep"), None),
        P(None, ("region", "rep")),
        P(),
        P(("region", "rep")),
        P(("region", "rep")),
        P("region", "rep", None, None),
        P("region", None, None),
        P("region", None, None),
    )
    return jax.shard_map(
        local,
        mesh=mesh,
        in_specs=placed,
        out_specs=(P(("region", "rep")), P("region", None)),
        check_vma=False,
    )
```

```python
import functools

import jax
import jax.numpy as jnp
from jax import lax
from jax.experimental import pallas as pl
from jax.experimental.pallas import tpu as pltpu
from jax.sharding import PartitionSpec as P

LAM = 0.25
F32 = jnp.float32
BF16 = jnp.bfloat16
TN = (((0,), (0,)), ((), ()))


def trip_kernel(
    pair_count, trip_steps, pb_ref, len_ref, inc_ref, qt_ref, tgt_ref, w_ref, _, pred_ref, out_ref,
    acc_ref,
):
    step = pl.program_id(0)
    per_step = len_ref.shape[0]
    block = qt_ref.shape[0]

    @pl.when(step == 0)
    def _():
        acc_ref[...] = jnp.zeros_like(acc_ref)

    @pl.when(step < trip_steps)
    def _():
        for u in range(per_step):
            t = step * per_step + u
            hidden = None
            for k in range(0, pair_count, 2):
                p0 = pb_ref[t * pair_count + k]
                p1 = pb_ref[t * pair_count + k + 1]
                lhs = jnp.concatenate([len_ref[u, k], len_ref[u, k + 1]], axis=1)
                rhs = jnp.concatenate([inc_ref[p0], inc_ref[p1]], axis=0)
                term = jnp.dot(lhs, rhs, preferred_element_type=F32)
                hidden = term if hidden is None else hidden + term
            q_t = qt_ref[:, u * block : (u + 1) * block]
            pred_row = jnp.sum(hidden.T * q_t, axis=0, keepdims=True)
            pred_ref[u] = pred_row
            err_row = w_ref[u] * (pred_row - tgt_ref[u])
            scaled_t = (err_row * q_t).astype(BF16)
            for k in range(0, pair_count, 2):
                p0 = pb_ref[t * pair_count + k]
                p1 = pb_ref[t * pair_count + k + 1]
                rhs = jnp.concatenate([len_ref[u, k], len_ref[u, k + 1]], axis=1)
                both = jnp.dot(scaled_t, rhs, preferred_element_type=F32)
                acc_ref[p0] += both[:, :block]
                acc_ref[p1] += both[:, block:]

    @pl.when(step >= trip_steps)
    def _():
        chunk = out_ref.shape[0]
        first = pl.multiple_of((step - trip_steps) * chunk, chunk)
        out_ref[...] = acc_ref[pl.ds(first, chunk)].astype(out_ref.dtype)


def trip_pass(pair_flat, lengths, incoming, query_t, tgt, wts, after, per_step=8, flush=4):
    trip_blocks, pair_count, block, rank = lengths.shape
    slots = incoming.shape[0]
    trip_steps = trip_blocks // per_step
    chunk = slots // flush
    last = trip_steps - 1
    const3 = lambda t, pb: (0, 0, 0)
    return pl.pallas_call(
        functools.partial(trip_kernel, pair_count, trip_steps),
        grid_spec=pltpu.PrefetchScalarGridSpec(
            num_scalar_prefetch=1,
            grid=(trip_steps + flush,),
            in_specs=[
                pl.BlockSpec(
                    (per_step, pair_count, block, block),
                    lambda t, pb: (jnp.minimum(t, last), 0, 0, 0),
                ),
                pl.BlockSpec((slots, block, rank), const3, pipeline_mode=pl.Buffered(1)),
                pl.BlockSpec((rank, per_step * block), lambda t, pb: (0, jnp.minimum(t, last))),
                pl.BlockSpec((per_step, 1, block), lambda t, pb: (jnp.minimum(t, last), 0, 0)),
                pl.BlockSpec((per_step, 1, block), lambda t, pb: (jnp.minimum(t, last), 0, 0)),
                pl.BlockSpec(memory_space=pl.ANY),
            ],
            out_specs=[
                pl.BlockSpec((per_step, 1, block), lambda t, pb: (jnp.minimum(t, last), 0, 0)),
                pl.BlockSpec(
                    (chunk, block, rank), lambda t, pb: (jnp.maximum(t - trip_steps, 0), 0, 0)
                ),
            ],
            scratch_shapes=[pltpu.VMEM((slots, block, rank), F32)],
        ),
        out_shape=[
            jax.ShapeDtypeStruct((trip_blocks, 1, block), F32),
            jax.ShapeDtypeStruct((slots, block, rank), BF16),
        ],
        compiler_params=pltpu.CompilerParams(
            dimension_semantics=("arbitrary",), vmem_limit_bytes=60 * 1024 * 1024
        ),
    )(pair_flat, lengths, incoming, query_t, tgt, wts, after)


def band_of(nb_ref, w_ref, base, rows):
    span = 3 * rows
    row = lax.broadcasted_iota(jnp.int32, (span, rows), 0)
    band = jnp.zeros((span, rows), F32)
    for k in range(nb_ref.shape[0]):
        rel = nb_ref[k : k + 1, :] - base
        band = band - jnp.where(row == rel, w_ref[k : k + 1, :], 0.0)
    mid_row = lax.broadcasted_iota(jnp.int32, (rows, rows), 0)
    mid_col = lax.broadcasted_iota(jnp.int32, (rows, rows), 1)
    total = jnp.sum(w_ref[...], axis=0, keepdims=True)
    mid = band[rows : 2 * rows] + jnp.where(mid_row == mid_col, total, 0.0)
    band = jnp.concatenate([band[:rows], mid, band[2 * rows :]], axis=0)
    hi = band.astype(BF16)
    lo = (band - hi.astype(F32)).astype(BF16)
    return hi, lo


def apply_band(hi, lo, window):
    return lax.dot_general(hi, window, TN, preferred_element_type=F32) + lax.dot_general(
        lo, window, TN, preferred_element_type=F32
    )


def smooth_inner_kernel(emb_ref, nb_ref, w_ref, out_ref):
    rows = out_ref.shape[0]
    i = pl.program_id(0) + 1
    hi, lo = band_of(nb_ref, w_ref, i * rows, rows)
    window = emb_ref[pl.ds(pl.multiple_of((i - 1) * rows, rows), 3 * rows), :]
    out_ref[...] = apply_band(hi, lo, window)


def smooth_edge_kernel(last, win_ref, nb_ref, w_ref, out_ref):
    rows = out_ref.shape[0]
    i = pl.program_id(0) * last
    hi, lo = band_of(nb_ref, w_ref, i * rows, rows)
    out_ref[...] = apply_band(hi, lo, win_ref[0])


def smooth_inner(emb, nb_t, w_t, rows):
    seg_rows, rank = emb.shape
    inner = seg_rows // rows - 2
    return pl.pallas_call(
        smooth_inner_kernel,
        grid=(inner,),
        in_specs=[
            pl.BlockSpec(emb.shape, lambda i: (0, 0), pipeline_mode=pl.Buffered(1)),
            pl.BlockSpec((nb_t.shape[0], rows), lambda i: (0, i + 1)),
            pl.BlockSpec((w_t.shape[0], rows), lambda i: (0, i + 1)),
        ],
        out_specs=pl.BlockSpec((rows, rank), lambda i: (i, 0)),
        out_shape=jax.ShapeDtypeStruct((inner * rows, rank), F32),
        compiler_params=pltpu.CompilerParams(dimension_semantics=("arbitrary",)),
    )(emb, nb_t, w_t)


def smooth_edge(windows, nb_t, w_t, rows):
    rank = windows.shape[2]
    last = nb_t.shape[1] // rows - 1
    return pl.pallas_call(
        functools.partial(smooth_edge_kernel, last),
        grid=(2,),
        in_specs=[
            pl.BlockSpec((1,) + windows.shape[1:], lambda i: (i, 0, 0)),
            pl.BlockSpec((nb_t.shape[0], rows), lambda i: (0, i * last)),
            pl.BlockSpec((w_t.shape[0], rows), lambda i: (0, i * last)),
        ],
        out_specs=pl.BlockSpec((rows, rank), lambda i: (i, 0)),
        out_shape=jax.ShapeDtypeStruct((2 * rows, rank), F32),
        compiler_params=pltpu.CompilerParams(dimension_semantics=("arbitrary",)),
    )(windows, nb_t, w_t)


def owned_kernel(tgt_ref, ret_ref, _, out_ref):
    c = pl.program_id(0)
    chunk = ret_ref.shape[0]

    @pl.when(c == 0)
    def _():
        out_ref[...] = jnp.zeros_like(out_ref)

    for s in range(chunk):
        b = tgt_ref[c * chunk + s]

        @pl.when(b >= 0)
        def _():
            out_ref[b] += ret_ref[s].astype(F32)

    @pl.when(c == pl.num_programs(0) - 1)
    def _():
        for b in range(out_ref.shape[0]):
            out_ref[b] = out_ref[b].T


def owned_pass(targets, returned, after, block_count, chunk=128):
    slots, rank, block = returned.shape
    return pl.pallas_call(
        owned_kernel,
        grid_spec=pltpu.PrefetchScalarGridSpec(
            num_scalar_prefetch=1,
            grid=(slots // chunk,),
            in_specs=[
                pl.BlockSpec((chunk, rank, block), lambda c, tg: (c, 0, 0)),
                pl.BlockSpec(memory_space=pl.ANY),
            ],
            out_specs=pl.BlockSpec(
                (block_count, rank, block), lambda c, tg: (0, 0, 0), pipeline_mode=pl.Buffered(1)
            ),
        ),
        out_shape=jax.ShapeDtypeStruct((block_count, rank, block), F32),
        compiler_params=pltpu.CompilerParams(dimension_semantics=("arbitrary",)),
    )(targets, returned, after)


def gather_kernel(idx_ref, src_ref, out_ref):
    c = pl.program_id(0)
    chunk = out_ref.shape[0]
    for s in range(chunk):
        out_ref[s] = src_ref[idx_ref[c * chunk + s]]


def gather_blocks(idx, blocks, chunk=128):
    count = idx.shape[0]
    return pl.pallas_call(
        gather_kernel,
        grid_spec=pltpu.PrefetchScalarGridSpec(
            num_scalar_prefetch=1,
            grid=(count // chunk,),
            in_specs=[
                pl.BlockSpec(blocks.shape, lambda c, ix: (0, 0, 0), pipeline_mode=pl.Buffered(1))
            ],
            out_specs=pl.BlockSpec((chunk,) + blocks.shape[1:], lambda c, ix: (c, 0, 0)),
        ),
        out_shape=jax.ShapeDtypeStruct((count,) + blocks.shape[1:], blocks.dtype),
    )(idx, blocks)


def local(
    emb, lengths, pair_block, feats, proj, targets, trip_weight, send_list, nb_index, nb_weight
):
    block_size = lengths.shape[2]
    rank_width = emb.shape[1]
    seg_rows = emb.shape[0]
    block_count = seg_rows // block_size
    regions = lax.axis_size("region")
    blocks = emb.reshape(block_count, block_size, rank_width)
    send_rows = send_list[0, 0]
    live_mask = send_rows >= 0
    slot_count = send_rows.shape[1]
    outgoing = gather_blocks(jnp.where(live_mask, send_rows, 0).reshape(-1), blocks)
    outgoing = outgoing.reshape(regions, slot_count, block_size, rank_width)
    incoming = lax.all_to_all(outgoing, "region", split_axis=0, concat_axis=0, tiled=True)
    incoming = incoming.reshape(regions * slot_count, block_size, rank_width)
    trip_blocks = lengths.shape[0]
    query_t = jnp.einsum("fr,ft->rt", proj, feats, preferred_element_type=F32)

    nb_t = nb_index[0]
    w_t = nb_weight[0]
    inner = smooth_inner(emb, nb_t, w_t, block_size)
    count = regions
    head = emb[:block_size]
    tail = emb[seg_rows - block_size :]
    prev_tail = lax.ppermute(tail, "region", [(i, (i + 1) % count) for i in range(count)])
    next_head = lax.ppermute(head, "region", [((i + 1) % count, i) for i in range(count)])
    windows = jnp.stack(
        [
            jnp.concatenate([prev_tail, emb[: 2 * block_size]], axis=0),
            jnp.concatenate([emb[seg_rows - 2 * block_size :], next_head], axis=0),
        ]
    )
    edge = smooth_edge(windows, nb_t, w_t, block_size)

    pred_rows, slot_grad = trip_pass(
        pair_block.reshape(-1),
        lengths,
        incoming,
        query_t,
        targets.reshape(trip_blocks, 1, block_size),
        trip_weight.reshape(trip_blocks, 1, block_size),
        inner,
    )
    predicted = pred_rows.reshape(trip_blocks * block_size)

    returned = lax.all_to_all(
        slot_grad.reshape(regions, slot_count, rank_width, block_size),
        "region",
        split_axis=0,
        concat_axis=0,
        tiled=True,
    )
    returned = returned.reshape(regions * slot_count, rank_width, block_size)

    target_rows = jnp.where(live_mask, send_rows, -1).reshape(-1)
    owned = owned_pass(target_rows, returned, edge, block_count).reshape(seg_rows, rank_width)
    partner = lax.ppermute(owned, "rep", [(0, 1), (1, 0)])
    smoothed = jnp.concatenate([edge[:block_size], inner, edge[block_size:]], axis=0)
    gradient = (owned + partner) + LAM * smoothed
    return (predicted, gradient.astype(jnp.bfloat16))


def solution(mesh):
    placed = (
        P("region", None),
        P(("region", "rep"), None, None, None),
        P(("region", "rep"), None),
        P(None, ("region", "rep")),
        P(),
        P(("region", "rep")),
        P(("region", "rep")),
        P("region", "rep", None, None),
        P("region", None, None),
        P("region", None, None),
    )
    return jax.shard_map(
        local,
        mesh=mesh,
        in_specs=placed,
        out_specs=(P(("region", "rep")), P("region", None)),
        check_vma=False,
    )
```

```python
import functools

import jax
import jax.numpy as jnp
from jax import lax
from jax.experimental import pallas as pl
from jax.experimental.pallas import tpu as pltpu
from jax.sharding import PartitionSpec as P

LAM = 0.25
F32 = jnp.float32
BF16 = jnp.bfloat16
TN = (((0,), (0,)), ((), ()))


def trip_kernel(
    pair_count, trip_steps, pb_ref, len_ref, inc_hbm, qt_ref, tgt_ref, w_ref, _, pred_ref, out_ref,
    acc_ref, inc_ref, inc_sem,
):
    step = pl.program_id(0)
    per_step = len_ref.shape[0]
    block = qt_ref.shape[0]

    @pl.when(step == 0)
    def _():
        copy = pltpu.make_async_copy(inc_hbm, inc_ref, inc_sem)
        copy.start()
        acc_ref[...] = jnp.zeros_like(acc_ref)
        copy.wait()

    @pl.when(step < trip_steps)
    def _():
        for u in range(per_step):
            t = step * per_step + u
            hidden = None
            for k in range(0, pair_count, 2):
                p0 = pb_ref[t * pair_count + k]
                p1 = pb_ref[t * pair_count + k + 1]
                lhs = jnp.concatenate([len_ref[u, k], len_ref[u, k + 1]], axis=1)
                rhs = jnp.concatenate([inc_ref[p0], inc_ref[p1]], axis=0)
                term = jnp.dot(lhs, rhs, preferred_element_type=F32)
                hidden = term if hidden is None else hidden + term
            q_t = qt_ref[:, u * block : (u + 1) * block]
            pred_row = jnp.sum(hidden.T * q_t, axis=0, keepdims=True)
            pred_ref[u] = pred_row
            err_row = w_ref[u] * (pred_row - tgt_ref[u])
            scaled_t = (err_row * q_t).astype(BF16)
            for k in range(0, pair_count, 2):
                p0 = pb_ref[t * pair_count + k]
                p1 = pb_ref[t * pair_count + k + 1]
                rhs = jnp.concatenate([len_ref[u, k], len_ref[u, k + 1]], axis=1)
                both = jnp.dot(scaled_t, rhs, preferred_element_type=F32)
                acc_ref[p0] += both[:, :block]
                acc_ref[p1] += both[:, block:]

    @pl.when(step >= trip_steps)
    def _():
        chunk = out_ref.shape[0]
        first = pl.multiple_of((step - trip_steps) * chunk, chunk)
        out_ref[...] = acc_ref[pl.ds(first, chunk)].astype(out_ref.dtype)


def trip_pass(pair_flat, lengths, incoming, query_t, tgt, wts, after, per_step=8, flush=4):
    trip_blocks, pair_count, block, rank = lengths.shape
    slots = incoming.shape[0]
    trip_steps = trip_blocks // per_step
    chunk = slots // flush
    last = trip_steps - 1
    return pl.pallas_call(
        functools.partial(trip_kernel, pair_count, trip_steps),
        grid_spec=pltpu.PrefetchScalarGridSpec(
            num_scalar_prefetch=1,
            grid=(trip_steps + flush,),
            in_specs=[
                pl.BlockSpec(
                    (per_step, pair_count, block, block),
                    lambda t, pb: (jnp.minimum(t, last), 0, 0, 0),
                ),
                pl.BlockSpec(memory_space=pl.ANY),
                pl.BlockSpec((rank, per_step * block), lambda t, pb: (0, jnp.minimum(t, last))),
                pl.BlockSpec((per_step, 1, block), lambda t, pb: (jnp.minimum(t, last), 0, 0)),
                pl.BlockSpec((per_step, 1, block), lambda t, pb: (jnp.minimum(t, last), 0, 0)),
                pl.BlockSpec(memory_space=pl.ANY),
            ],
            out_specs=[
                pl.BlockSpec((per_step, 1, block), lambda t, pb: (jnp.minimum(t, last), 0, 0)),
                pl.BlockSpec(
                    (chunk, block, rank), lambda t, pb: (jnp.maximum(t - trip_steps, 0), 0, 0)
                ),
            ],
            scratch_shapes=[
                pltpu.VMEM((slots, block, rank), F32),
                pltpu.VMEM(incoming.shape, incoming.dtype),
                pltpu.SemaphoreType.DMA(()),
            ],
        ),
        out_shape=[
            jax.ShapeDtypeStruct((trip_blocks, 1, block), F32),
            jax.ShapeDtypeStruct((slots, block, rank), BF16),
        ],
        compiler_params=pltpu.CompilerParams(
            dimension_semantics=("arbitrary",), vmem_limit_bytes=60 * 1024 * 1024
        ),
    )(pair_flat, lengths, incoming, query_t, tgt, wts, after)


def band_of(nb_ref, w_ref, base, rows):
    span = 3 * rows
    row = lax.broadcasted_iota(jnp.int32, (span, rows), 0)
    band = jnp.zeros((span, rows), F32)
    for k in range(nb_ref.shape[0]):
        rel = nb_ref[k : k + 1, :] - base
        band = band - jnp.where(row == rel, w_ref[k : k + 1, :], 0.0)
    mid_row = lax.broadcasted_iota(jnp.int32, (rows, rows), 0)
    mid_col = lax.broadcasted_iota(jnp.int32, (rows, rows), 1)
    total = jnp.sum(w_ref[...], axis=0, keepdims=True)
    mid = band[rows : 2 * rows] + jnp.where(mid_row == mid_col, total, 0.0)
    band = jnp.concatenate([band[:rows], mid, band[2 * rows :]], axis=0)
    hi = band.astype(BF16)
    lo = (band - hi.astype(F32)).astype(BF16)
    return hi, lo


def apply_band(hi, lo, window):
    return lax.dot_general(hi, window, TN, preferred_element_type=F32) + lax.dot_general(
        lo, window, TN, preferred_element_type=F32
    )


def smooth_inner_kernel(emb_ref, nb_ref, w_ref, out_ref):
    rows = out_ref.shape[0]
    i = pl.program_id(0) + 1
    hi, lo = band_of(nb_ref, w_ref, i * rows, rows)
    window = emb_ref[pl.ds(pl.multiple_of((i - 1) * rows, rows), 3 * rows), :]
    out_ref[...] = apply_band(hi, lo, window)


def smooth_edge_kernel(last, win_ref, nb_ref, w_ref, out_ref):
    rows = out_ref.shape[0]
    i = pl.program_id(0) * last
    hi, lo = band_of(nb_ref, w_ref, i * rows, rows)
    out_ref[...] = apply_band(hi, lo, win_ref[0])


def smooth_inner(emb, nb_t, w_t, rows):
    seg_rows, rank = emb.shape
    inner = seg_rows // rows - 2
    return pl.pallas_call(
        smooth_inner_kernel,
        grid=(inner,),
        in_specs=[
            pl.BlockSpec(emb.shape, lambda i: (0, 0), pipeline_mode=pl.Buffered(1)),
            pl.BlockSpec((nb_t.shape[0], rows), lambda i: (0, i + 1)),
            pl.BlockSpec((w_t.shape[0], rows), lambda i: (0, i + 1)),
        ],
        out_specs=pl.BlockSpec((rows, rank), lambda i: (i, 0)),
        out_shape=jax.ShapeDtypeStruct((inner * rows, rank), F32),
        compiler_params=pltpu.CompilerParams(dimension_semantics=("arbitrary",)),
    )(emb, nb_t, w_t)


def smooth_edge(windows, nb_t, w_t, rows):
    rank = windows.shape[2]
    last = nb_t.shape[1] // rows - 1
    return pl.pallas_call(
        functools.partial(smooth_edge_kernel, last),
        grid=(2,),
        in_specs=[
            pl.BlockSpec((1,) + windows.shape[1:], lambda i: (i, 0, 0)),
            pl.BlockSpec((nb_t.shape[0], rows), lambda i: (0, i * last)),
            pl.BlockSpec((w_t.shape[0], rows), lambda i: (0, i * last)),
        ],
        out_specs=pl.BlockSpec((rows, rank), lambda i: (i, 0)),
        out_shape=jax.ShapeDtypeStruct((2 * rows, rank), F32),
        compiler_params=pltpu.CompilerParams(dimension_semantics=("arbitrary",)),
    )(windows, nb_t, w_t)


def owned_kernel(tgt_ref, ret_ref, _, out_ref):
    c = pl.program_id(0)
    chunk = ret_ref.shape[0]

    @pl.when(c == 0)
    def _():
        out_ref[...] = jnp.zeros_like(out_ref)

    for s in range(chunk):
        b = tgt_ref[c * chunk + s]

        @pl.when(b >= 0)
        def _():
            out_ref[b] += ret_ref[s].astype(F32)

    @pl.when(c == pl.num_programs(0) - 1)
    def _():
        for b in range(out_ref.shape[0]):
            out_ref[b] = out_ref[b].T


def owned_pass(targets, returned, after, block_count, chunk=128):
    slots, rank, block = returned.shape
    return pl.pallas_call(
        owned_kernel,
        grid_spec=pltpu.PrefetchScalarGridSpec(
            num_scalar_prefetch=1,
            grid=(slots // chunk,),
            in_specs=[
                pl.BlockSpec((chunk, rank, block), lambda c, tg: (c, 0, 0)),
                pl.BlockSpec(memory_space=pl.ANY),
            ],
            out_specs=pl.BlockSpec(
                (block_count, rank, block), lambda c, tg: (0, 0, 0), pipeline_mode=pl.Buffered(1)
            ),
        ),
        out_shape=jax.ShapeDtypeStruct((block_count, rank, block), F32),
        compiler_params=pltpu.CompilerParams(dimension_semantics=("arbitrary",)),
    )(targets, returned, after)


def gather_kernel(idx_ref, src_ref, out_ref):
    c = pl.program_id(0)
    chunk = out_ref.shape[0]
    for s in range(chunk):
        out_ref[s] = src_ref[idx_ref[c * chunk + s]]


def gather_blocks(idx, blocks, chunk=128):
    count = idx.shape[0]
    return pl.pallas_call(
        gather_kernel,
        grid_spec=pltpu.PrefetchScalarGridSpec(
            num_scalar_prefetch=1,
            grid=(count // chunk,),
            in_specs=[
                pl.BlockSpec(blocks.shape, lambda c, ix: (0, 0, 0), pipeline_mode=pl.Buffered(1))
            ],
            out_specs=pl.BlockSpec((chunk,) + blocks.shape[1:], lambda c, ix: (c, 0, 0)),
        ),
        out_shape=jax.ShapeDtypeStruct((count,) + blocks.shape[1:], blocks.dtype),
    )(idx, blocks)


def local(
    emb, lengths, pair_block, feats, proj, targets, trip_weight, send_list, nb_index, nb_weight
):
    block_size = lengths.shape[2]
    rank_width = emb.shape[1]
    seg_rows = emb.shape[0]
    block_count = seg_rows // block_size
    regions = lax.axis_size("region")
    blocks = emb.reshape(block_count, block_size, rank_width)
    send_rows = send_list[0, 0]
    live_mask = send_rows >= 0
    slot_count = send_rows.shape[1]
    outgoing = gather_blocks(jnp.where(live_mask, send_rows, 0).reshape(-1), blocks)
    outgoing = outgoing.reshape(regions, slot_count, block_size, rank_width)
    incoming = lax.all_to_all(outgoing, "region", split_axis=0, concat_axis=0, tiled=True)
    incoming = incoming.reshape(regions * slot_count, block_size, rank_width)
    trip_blocks = lengths.shape[0]
    query_t = jnp.einsum("fr,ft->rt", proj, feats, preferred_element_type=F32)

    nb_t = nb_index[0]
    w_t = nb_weight[0]
    inner = smooth_inner(emb, nb_t, w_t, block_size)
    count = regions
    head = emb[:block_size]
    tail = emb[seg_rows - block_size :]
    prev_tail = lax.ppermute(tail, "region", [(i, (i + 1) % count) for i in range(count)])
    next_head = lax.ppermute(head, "region", [((i + 1) % count, i) for i in range(count)])
    windows = jnp.stack(
        [
            jnp.concatenate([prev_tail, emb[: 2 * block_size]], axis=0),
            jnp.concatenate([emb[seg_rows - 2 * block_size :], next_head], axis=0),
        ]
    )
    edge = smooth_edge(windows, nb_t, w_t, block_size)

    pred_rows, slot_grad = trip_pass(
        pair_block.reshape(-1),
        lengths,
        incoming,
        query_t,
        targets.reshape(trip_blocks, 1, block_size),
        trip_weight.reshape(trip_blocks, 1, block_size),
        inner,
    )
    predicted = pred_rows.reshape(trip_blocks * block_size)

    returned = lax.all_to_all(
        slot_grad.reshape(regions, slot_count, rank_width, block_size),
        "region",
        split_axis=0,
        concat_axis=0,
        tiled=True,
    )
    returned = returned.reshape(regions * slot_count, rank_width, block_size)

    target_rows = jnp.where(live_mask, send_rows, -1).reshape(-1)
    owned = owned_pass(target_rows, returned, edge, block_count).reshape(seg_rows, rank_width)
    partner = lax.ppermute(owned, "rep", [(0, 1), (1, 0)])
    smoothed = jnp.concatenate([edge[:block_size], inner, edge[block_size:]], axis=0)
    gradient = (owned + partner) + LAM * smoothed
    return (predicted, gradient.astype(jnp.bfloat16))


def solution(mesh):
    placed = (
        P("region", None),
        P(("region", "rep"), None, None, None),
        P(("region", "rep"), None),
        P(None, ("region", "rep")),
        P(),
        P(("region", "rep")),
        P(("region", "rep")),
        P("region", "rep", None, None),
        P("region", None, None),
        P("region", None, None),
    )
    return jax.shard_map(
        local,
        mesh=mesh,
        in_specs=placed,
        out_specs=(P(("region", "rep")), P("region", None)),
        check_vma=False,
    )
```

```python
import functools

import jax
import jax.numpy as jnp
from jax import lax
from jax.experimental import pallas as pl
from jax.experimental.pallas import tpu as pltpu
from jax.sharding import PartitionSpec as P

LAM = 0.25
F32 = jnp.float32
BF16 = jnp.bfloat16
TN = (((0,), (0,)), ((), ()))


def trip_kernel(
    pair_count, trip_steps, pb_ref, len_ref, inc_ref, qt_ref, tgt_ref, w_ref, _, pred_ref, out_ref,
    acc_ref,
):
    step = pl.program_id(0)
    per_step = len_ref.shape[0]
    block = qt_ref.shape[0]

    @pl.when(step == 0)
    def _():
        acc_ref[...] = jnp.zeros_like(acc_ref)

    @pl.when(step < trip_steps)
    def _():
        for u in range(per_step):
            t = step * per_step + u
            hidden = None
            for k in range(0, pair_count, 2):
                p0 = pb_ref[t * pair_count + k]
                p1 = pb_ref[t * pair_count + k + 1]
                lhs = jnp.concatenate([len_ref[u, k], len_ref[u, k + 1]], axis=1)
                rhs = jnp.concatenate([inc_ref[p0], inc_ref[p1]], axis=0)
                term = jnp.dot(lhs, rhs, preferred_element_type=F32)
                hidden = term if hidden is None else hidden + term
            q_t = qt_ref[:, u * block : (u + 1) * block]
            pred_row = jnp.sum(hidden.T * q_t, axis=0, keepdims=True)
            pred_ref[u] = pred_row
            err_row = w_ref[u] * (pred_row - tgt_ref[u])
            scaled_t = (err_row * q_t).astype(BF16)
            for k in range(0, pair_count, 2):
                p0 = pb_ref[t * pair_count + k]
                p1 = pb_ref[t * pair_count + k + 1]
                rhs = jnp.concatenate([len_ref[u, k], len_ref[u, k + 1]], axis=1)
                both = jnp.dot(scaled_t, rhs, preferred_element_type=F32)
                acc_ref[p0] += both[:, :block]
                acc_ref[p1] += both[:, block:]

    @pl.when(step >= trip_steps)
    def _():
        chunk = out_ref.shape[0]
        first = pl.multiple_of((step - trip_steps) * chunk, chunk)
        out_ref[...] = acc_ref[pl.ds(first, chunk)].astype(out_ref.dtype)


def trip_pass(pair_flat, lengths, incoming, query_t, tgt, wts, after, per_step=8, flush=4):
    trip_blocks, pair_count, block, rank = lengths.shape
    slots = incoming.shape[0]
    trip_steps = trip_blocks // per_step
    chunk = slots // flush
    last = trip_steps - 1
    const3 = lambda t, pb: (0, 0, 0)
    return pl.pallas_call(
        functools.partial(trip_kernel, pair_count, trip_steps),
        grid_spec=pltpu.PrefetchScalarGridSpec(
            num_scalar_prefetch=1,
            grid=(trip_steps + flush,),
            in_specs=[
                pl.BlockSpec(
                    (per_step, pair_count, block, block),
                    lambda t, pb: (jnp.minimum(t, last), 0, 0, 0),
                ),
                pl.BlockSpec((slots, block, rank), const3, pipeline_mode=pl.Buffered(1)),
                pl.BlockSpec((rank, per_step * block), lambda t, pb: (0, jnp.minimum(t, last))),
                pl.BlockSpec((per_step, 1, block), lambda t, pb: (jnp.minimum(t, last), 0, 0)),
                pl.BlockSpec((per_step, 1, block), lambda t, pb: (jnp.minimum(t, last), 0, 0)),
                pl.BlockSpec(memory_space=pl.ANY),
            ],
            out_specs=[
                pl.BlockSpec((per_step, 1, block), lambda t, pb: (jnp.minimum(t, last), 0, 0)),
                pl.BlockSpec(
                    (chunk, block, rank), lambda t, pb: (jnp.maximum(t - trip_steps, 0), 0, 0)
                ),
            ],
            scratch_shapes=[pltpu.VMEM((slots, block, rank), F32)],
        ),
        out_shape=[
            jax.ShapeDtypeStruct((trip_blocks, 1, block), F32),
            jax.ShapeDtypeStruct((slots, block, rank), BF16),
        ],
        compiler_params=pltpu.CompilerParams(
            dimension_semantics=("arbitrary",), vmem_limit_bytes=60 * 1024 * 1024
        ),
    )(pair_flat, lengths, incoming, query_t, tgt, wts, after)


def band_of(nb_ref, w_ref, base, rows):
    span = 3 * rows
    row = lax.broadcasted_iota(jnp.int32, (span, rows), 0)
    band = jnp.zeros((span, rows), F32)
    for k in range(nb_ref.shape[0]):
        rel = nb_ref[k : k + 1, :] - base
        band = band - jnp.where(row == rel, w_ref[k : k + 1, :], 0.0)
    mid_row = lax.broadcasted_iota(jnp.int32, (rows, rows), 0)
    mid_col = lax.broadcasted_iota(jnp.int32, (rows, rows), 1)
    total = jnp.sum(w_ref[...], axis=0, keepdims=True)
    mid = band[rows : 2 * rows] + jnp.where(mid_row == mid_col, total, 0.0)
    band = jnp.concatenate([band[:rows], mid, band[2 * rows :]], axis=0)
    hi = band.astype(BF16)
    lo = (band - hi.astype(F32)).astype(BF16)
    return hi, lo


def apply_band(hi, lo, window):
    return lax.dot_general(hi, window, TN, preferred_element_type=F32) + lax.dot_general(
        lo, window, TN, preferred_element_type=F32
    )


def smooth_inner_kernel(emb_ref, nb_ref, w_ref, out_ref):
    rows = out_ref.shape[0]
    i = pl.program_id(0) + 1
    hi, lo = band_of(nb_ref, w_ref, i * rows, rows)
    window = emb_ref[pl.ds(pl.multiple_of((i - 1) * rows, rows), 3 * rows), :]
    out_ref[...] = apply_band(hi, lo, window)


def smooth_edge_kernel(last, win_ref, nb_ref, w_ref, out_ref):
    rows = out_ref.shape[0]
    i = pl.program_id(0) * last
    hi, lo = band_of(nb_ref, w_ref, i * rows, rows)
    out_ref[...] = apply_band(hi, lo, win_ref[0])


def smooth_inner(emb, nb_t, w_t, rows):
    seg_rows, rank = emb.shape
    inner = seg_rows // rows - 2
    return pl.pallas_call(
        smooth_inner_kernel,
        grid=(inner,),
        in_specs=[
            pl.BlockSpec(emb.shape, lambda i: (0, 0), pipeline_mode=pl.Buffered(1)),
            pl.BlockSpec((nb_t.shape[0], rows), lambda i: (0, i + 1)),
            pl.BlockSpec((w_t.shape[0], rows), lambda i: (0, i + 1)),
        ],
        out_specs=pl.BlockSpec((rows, rank), lambda i: (i, 0)),
        out_shape=jax.ShapeDtypeStruct((inner * rows, rank), F32),
        compiler_params=pltpu.CompilerParams(dimension_semantics=("arbitrary",)),
    )(emb, nb_t, w_t)


def smooth_edge(windows, nb_t, w_t, rows):
    rank = windows.shape[2]
    last = nb_t.shape[1] // rows - 1
    return pl.pallas_call(
        functools.partial(smooth_edge_kernel, last),
        grid=(2,),
        in_specs=[
            pl.BlockSpec((1,) + windows.shape[1:], lambda i: (i, 0, 0)),
            pl.BlockSpec((nb_t.shape[0], rows), lambda i: (0, i * last)),
            pl.BlockSpec((w_t.shape[0], rows), lambda i: (0, i * last)),
        ],
        out_specs=pl.BlockSpec((rows, rank), lambda i: (i, 0)),
        out_shape=jax.ShapeDtypeStruct((2 * rows, rank), F32),
        compiler_params=pltpu.CompilerParams(dimension_semantics=("arbitrary",)),
    )(windows, nb_t, w_t)


def owned_kernel(tgt_ref, ret_ref, _, out_ref):
    c = pl.program_id(0)
    chunk = ret_ref.shape[0]

    @pl.when(c == 0)
    def _():
        out_ref[...] = jnp.zeros_like(out_ref)

    for s in range(chunk):
        b = tgt_ref[c * chunk + s]

        @pl.when(b >= 0)
        def _():
            out_ref[b] += ret_ref[s].astype(F32)

    @pl.when(c == pl.num_programs(0) - 1)
    def _():
        for b in range(out_ref.shape[0]):
            out_ref[b] = out_ref[b].T


def owned_pass(targets, returned, after, block_count, chunk=128):
    slots, rank, block = returned.shape
    return pl.pallas_call(
        owned_kernel,
        grid_spec=pltpu.PrefetchScalarGridSpec(
            num_scalar_prefetch=1,
            grid=(slots // chunk,),
            in_specs=[
                pl.BlockSpec((chunk, rank, block), lambda c, tg: (c, 0, 0)),
                pl.BlockSpec(memory_space=pl.ANY),
            ],
            out_specs=pl.BlockSpec(
                (block_count, rank, block), lambda c, tg: (0, 0, 0), pipeline_mode=pl.Buffered(1)
            ),
        ),
        out_shape=jax.ShapeDtypeStruct((block_count, rank, block), F32),
        compiler_params=pltpu.CompilerParams(dimension_semantics=("arbitrary",)),
    )(targets, returned, after)


def gather_kernel(idx_ref, src_ref, out_ref):
    c = pl.program_id(0)
    chunk = out_ref.shape[0]
    for s in range(chunk):
        out_ref[s] = src_ref[idx_ref[c * chunk + s]]


def gather_blocks(idx, blocks, chunk=128):
    count = idx.shape[0]
    return pl.pallas_call(
        gather_kernel,
        grid_spec=pltpu.PrefetchScalarGridSpec(
            num_scalar_prefetch=1,
            grid=(count // chunk,),
            in_specs=[
                pl.BlockSpec(blocks.shape, lambda c, ix: (0, 0, 0), pipeline_mode=pl.Buffered(1))
            ],
            out_specs=pl.BlockSpec((chunk,) + blocks.shape[1:], lambda c, ix: (c, 0, 0)),
        ),
        out_shape=jax.ShapeDtypeStruct((count,) + blocks.shape[1:], blocks.dtype),
    )(idx, blocks)


def local(
    emb, lengths, pair_block, feats, proj, targets, trip_weight, send_list, nb_index, nb_weight
):
    block_size = lengths.shape[2]
    rank_width = emb.shape[1]
    seg_rows = emb.shape[0]
    block_count = seg_rows // block_size
    regions = lax.axis_size("region")
    blocks = emb.reshape(block_count, block_size, rank_width)
    send_rows = send_list[0, 0]
    live_mask = send_rows >= 0
    slot_count = send_rows.shape[1]
    outgoing = gather_blocks(jnp.where(live_mask, send_rows, 0).reshape(-1), blocks)
    outgoing = outgoing.reshape(regions, slot_count, block_size, rank_width)
    incoming = lax.all_to_all(outgoing, "region", split_axis=0, concat_axis=0, tiled=True)
    incoming = incoming.reshape(regions * slot_count, block_size, rank_width)
    trip_blocks = lengths.shape[0]
    query_t = jnp.einsum("fr,ft->rt", proj, feats, preferred_element_type=F32)

    nb_t = nb_index[0]
    w_t = nb_weight[0]
    inner = smooth_inner(emb, nb_t, w_t, block_size)

    pred_rows, slot_grad = trip_pass(
        pair_block.reshape(-1),
        lengths,
        incoming,
        query_t,
        targets.reshape(trip_blocks, 1, block_size),
        trip_weight.reshape(trip_blocks, 1, block_size),
        inner,
    )
    predicted = pred_rows.reshape(trip_blocks * block_size)

    returned = lax.all_to_all(
        slot_grad.reshape(regions, slot_count, rank_width, block_size),
        "region",
        split_axis=0,
        concat_axis=0,
        tiled=True,
    )
    returned = returned.reshape(regions * slot_count, rank_width, block_size)
    count = regions
    returned, head, tail = lax.optimization_barrier(
        (returned, emb[:block_size], emb[seg_rows - block_size :])
    )
    prev_tail = lax.ppermute(tail, "region", [(i, (i + 1) % count) for i in range(count)])
    next_head = lax.ppermute(head, "region", [((i + 1) % count, i) for i in range(count)])
    windows = jnp.stack(
        [
            jnp.concatenate([prev_tail, emb[: 2 * block_size]], axis=0),
            jnp.concatenate([emb[seg_rows - 2 * block_size :], next_head], axis=0),
        ]
    )
    edge = smooth_edge(windows, nb_t, w_t, block_size)

    target_rows = jnp.where(live_mask, send_rows, -1).reshape(-1)
    owned = owned_pass(target_rows, returned, inner, block_count).reshape(seg_rows, rank_width)
    partner = lax.ppermute(owned, "rep", [(0, 1), (1, 0)])
    smoothed = jnp.concatenate([edge[:block_size], inner, edge[block_size:]], axis=0)
    gradient = (owned + partner) + LAM * smoothed
    return (predicted, gradient.astype(jnp.bfloat16))


def solution(mesh):
    placed = (
        P("region", None),
        P(("region", "rep"), None, None, None),
        P(("region", "rep"), None),
        P(None, ("region", "rep")),
        P(),
        P(("region", "rep")),
        P(("region", "rep")),
        P("region", "rep", None, None),
        P("region", None, None),
        P("region", None, None),
    )
    return jax.shard_map(
        local,
        mesh=mesh,
        in_specs=placed,
        out_specs=(P(("region", "rep")), P("region", None)),
        check_vma=False,
    )
```

```python
import functools

import jax
import jax.numpy as jnp
from jax import lax
from jax.experimental import pallas as pl
from jax.experimental.pallas import tpu as pltpu
from jax.sharding import PartitionSpec as P

LAM = 0.25
F32 = jnp.float32
BF16 = jnp.bfloat16
TN = (((0,), (0,)), ((), ()))


def trip_kernel(
    pair_count, trip_steps, pb_ref, len_ref, inc_ref, qt_ref, tgt_ref, w_ref, _, pred_ref, out_ref,
    acc_ref,
):
    step = pl.program_id(0)
    per_step = len_ref.shape[0]
    block = qt_ref.shape[0]

    @pl.when(step == 0)
    def _():
        acc_ref[...] = jnp.zeros_like(acc_ref)

    @pl.when(step < trip_steps)
    def _():
        for u in range(per_step):
            t = step * per_step + u
            hidden = None
            for k in range(0, pair_count, 2):
                p0 = pb_ref[t * pair_count + k]
                p1 = pb_ref[t * pair_count + k + 1]
                lhs = jnp.concatenate([len_ref[u, k], len_ref[u, k + 1]], axis=1)
                rhs = jnp.concatenate([inc_ref[p0], inc_ref[p1]], axis=0)
                term = jnp.dot(lhs, rhs, preferred_element_type=F32)
                hidden = term if hidden is None else hidden + term
            q_t = qt_ref[:, u * block : (u + 1) * block]
            pred_row = jnp.sum(hidden.T * q_t, axis=0, keepdims=True)
            pred_ref[u] = pred_row
            err_row = w_ref[u] * (pred_row - tgt_ref[u])
            scaled_t = (err_row * q_t).astype(BF16)
            for k in range(0, pair_count, 2):
                p0 = pb_ref[t * pair_count + k]
                p1 = pb_ref[t * pair_count + k + 1]
                rhs = jnp.concatenate([len_ref[u, k], len_ref[u, k + 1]], axis=1)
                both = jnp.dot(scaled_t, rhs, preferred_element_type=F32)
                acc_ref[p0] += both[:, :block]
                acc_ref[p1] += both[:, block:]

    @pl.when(step >= trip_steps)
    def _():
        chunk = out_ref.shape[0]
        first = pl.multiple_of((step - trip_steps) * chunk, chunk)
        out_ref[...] = acc_ref[pl.ds(first, chunk)].astype(out_ref.dtype)


def trip_pass(pair_flat, lengths, incoming, query_t, tgt, wts, after, per_step=12, flush=4):
    trip_blocks, pair_count, block, rank = lengths.shape
    slots = incoming.shape[0]
    trip_steps = trip_blocks // per_step
    chunk = slots // flush
    last = trip_steps - 1
    const3 = lambda t, pb: (0, 0, 0)
    return pl.pallas_call(
        functools.partial(trip_kernel, pair_count, trip_steps),
        grid_spec=pltpu.PrefetchScalarGridSpec(
            num_scalar_prefetch=1,
            grid=(trip_steps + flush,),
            in_specs=[
                pl.BlockSpec(
                    (per_step, pair_count, block, block),
                    lambda t, pb: (jnp.minimum(t, last), 0, 0, 0),
                ),
                pl.BlockSpec((slots, block, rank), const3, pipeline_mode=pl.Buffered(1)),
                pl.BlockSpec((rank, per_step * block), lambda t, pb: (0, jnp.minimum(t, last))),
                pl.BlockSpec((per_step, 1, block), lambda t, pb: (jnp.minimum(t, last), 0, 0)),
                pl.BlockSpec((per_step, 1, block), lambda t, pb: (jnp.minimum(t, last), 0, 0)),
                pl.BlockSpec(memory_space=pl.ANY),
            ],
            out_specs=[
                pl.BlockSpec((per_step, 1, block), lambda t, pb: (jnp.minimum(t, last), 0, 0)),
                pl.BlockSpec(
                    (chunk, block, rank), lambda t, pb: (jnp.maximum(t - trip_steps, 0), 0, 0)
                ),
            ],
            scratch_shapes=[pltpu.VMEM((slots, block, rank), F32)],
        ),
        out_shape=[
            jax.ShapeDtypeStruct((trip_blocks, 1, block), F32),
            jax.ShapeDtypeStruct((slots, block, rank), BF16),
        ],
        compiler_params=pltpu.CompilerParams(
            dimension_semantics=("arbitrary",), vmem_limit_bytes=60 * 1024 * 1024
        ),
    )(pair_flat, lengths, incoming, query_t, tgt, wts, after)


def band_of(nb_ref, w_ref, base, rows):
    span = 3 * rows
    row = lax.broadcasted_iota(jnp.int32, (span, rows), 0)
    band = jnp.zeros((span, rows), F32)
    for k in range(nb_ref.shape[0]):
        rel = nb_ref[k : k + 1, :] - base
        band = band - jnp.where(row == rel, w_ref[k : k + 1, :], 0.0)
    mid_row = lax.broadcasted_iota(jnp.int32, (rows, rows), 0)
    mid_col = lax.broadcasted_iota(jnp.int32, (rows, rows), 1)
    total = jnp.sum(w_ref[...], axis=0, keepdims=True)
    mid = band[rows : 2 * rows] + jnp.where(mid_row == mid_col, total, 0.0)
    band = jnp.concatenate([band[:rows], mid, band[2 * rows :]], axis=0)
    hi = band.astype(BF16)
    lo = (band - hi.astype(F32)).astype(BF16)
    return hi, lo


def apply_band(hi, lo, window):
    return lax.dot_general(hi, window, TN, preferred_element_type=F32) + lax.dot_general(
        lo, window, TN, preferred_element_type=F32
    )


def smooth_inner_kernel(emb_ref, nb_ref, w_ref, out_ref):
    rows = out_ref.shape[0]
    i = pl.program_id(0) + 1
    hi, lo = band_of(nb_ref, w_ref, i * rows, rows)
    window = emb_ref[pl.ds(pl.multiple_of((i - 1) * rows, rows), 3 * rows), :]
    out_ref[...] = apply_band(hi, lo, window)


def smooth_edge_kernel(last, win_ref, nb_ref, w_ref, out_ref):
    rows = out_ref.shape[0]
    i = pl.program_id(0) * last
    hi, lo = band_of(nb_ref, w_ref, i * rows, rows)
    out_ref[...] = apply_band(hi, lo, win_ref[0])


def smooth_inner(emb, nb_t, w_t, rows):
    seg_rows, rank = emb.shape
    inner = seg_rows // rows - 2
    return pl.pallas_call(
        smooth_inner_kernel,
        grid=(inner,),
        in_specs=[
            pl.BlockSpec(emb.shape, lambda i: (0, 0), pipeline_mode=pl.Buffered(1)),
            pl.BlockSpec((nb_t.shape[0], rows), lambda i: (0, i + 1)),
            pl.BlockSpec((w_t.shape[0], rows), lambda i: (0, i + 1)),
        ],
        out_specs=pl.BlockSpec((rows, rank), lambda i: (i, 0)),
        out_shape=jax.ShapeDtypeStruct((inner * rows, rank), F32),
        compiler_params=pltpu.CompilerParams(dimension_semantics=("arbitrary",)),
    )(emb, nb_t, w_t)


def smooth_edge(windows, nb_t, w_t, rows):
    rank = windows.shape[2]
    last = nb_t.shape[1] // rows - 1
    return pl.pallas_call(
        functools.partial(smooth_edge_kernel, last),
        grid=(2,),
        in_specs=[
            pl.BlockSpec((1,) + windows.shape[1:], lambda i: (i, 0, 0)),
            pl.BlockSpec((nb_t.shape[0], rows), lambda i: (0, i * last)),
            pl.BlockSpec((w_t.shape[0], rows), lambda i: (0, i * last)),
        ],
        out_specs=pl.BlockSpec((rows, rank), lambda i: (i, 0)),
        out_shape=jax.ShapeDtypeStruct((2 * rows, rank), F32),
        compiler_params=pltpu.CompilerParams(dimension_semantics=("arbitrary",)),
    )(windows, nb_t, w_t)


def owned_kernel(tgt_ref, ret_ref, _, out_ref):
    c = pl.program_id(0)
    chunk = ret_ref.shape[0]

    @pl.when(c == 0)
    def _():
        out_ref[...] = jnp.zeros_like(out_ref)

    for s in range(chunk):
        b = tgt_ref[c * chunk + s]

        @pl.when(b >= 0)
        def _():
            out_ref[b] += ret_ref[s].astype(F32)

    @pl.when(c == pl.num_programs(0) - 1)
    def _():
        for b in range(out_ref.shape[0]):
            out_ref[b] = out_ref[b].T


def owned_pass(targets, returned, after, block_count, chunk=128):
    slots, rank, block = returned.shape
    return pl.pallas_call(
        owned_kernel,
        grid_spec=pltpu.PrefetchScalarGridSpec(
            num_scalar_prefetch=1,
            grid=(slots // chunk,),
            in_specs=[
                pl.BlockSpec((chunk, rank, block), lambda c, tg: (c, 0, 0)),
                pl.BlockSpec(memory_space=pl.ANY),
            ],
            out_specs=pl.BlockSpec(
                (block_count, rank, block), lambda c, tg: (0, 0, 0), pipeline_mode=pl.Buffered(1)
            ),
        ),
        out_shape=jax.ShapeDtypeStruct((block_count, rank, block), F32),
        compiler_params=pltpu.CompilerParams(dimension_semantics=("arbitrary",)),
    )(targets, returned, after)


def gather_kernel(idx_ref, src_ref, out_ref):
    c = pl.program_id(0)
    chunk = out_ref.shape[0]
    for s in range(chunk):
        out_ref[s] = src_ref[idx_ref[c * chunk + s]]


def gather_blocks(idx, blocks, chunk=128):
    count = idx.shape[0]
    return pl.pallas_call(
        gather_kernel,
        grid_spec=pltpu.PrefetchScalarGridSpec(
            num_scalar_prefetch=1,
            grid=(count // chunk,),
            in_specs=[
                pl.BlockSpec(blocks.shape, lambda c, ix: (0, 0, 0), pipeline_mode=pl.Buffered(1))
            ],
            out_specs=pl.BlockSpec((chunk,) + blocks.shape[1:], lambda c, ix: (c, 0, 0)),
        ),
        out_shape=jax.ShapeDtypeStruct((count,) + blocks.shape[1:], blocks.dtype),
    )(idx, blocks)


def local(
    emb, lengths, pair_block, feats, proj, targets, trip_weight, send_list, nb_index, nb_weight
):
    block_size = lengths.shape[2]
    rank_width = emb.shape[1]
    seg_rows = emb.shape[0]
    block_count = seg_rows // block_size
    regions = lax.axis_size("region")
    blocks = emb.reshape(block_count, block_size, rank_width)
    send_rows = send_list[0, 0]
    live_mask = send_rows >= 0
    slot_count = send_rows.shape[1]
    outgoing = gather_blocks(jnp.where(live_mask, send_rows, 0).reshape(-1), blocks)
    outgoing = outgoing.reshape(regions, slot_count, block_size, rank_width)
    incoming = lax.all_to_all(outgoing, "region", split_axis=0, concat_axis=0, tiled=True)
    incoming = incoming.reshape(regions * slot_count, block_size, rank_width)
    trip_blocks = lengths.shape[0]
    query_t = jnp.einsum("fr,ft->rt", proj, feats, preferred_element_type=F32)

    nb_t = nb_index[0]
    w_t = nb_weight[0]
    inner = smooth_inner(emb, nb_t, w_t, block_size)
    count = regions
    head = emb[:block_size]
    tail = emb[seg_rows - block_size :]
    prev_tail = lax.ppermute(tail, "region", [(i, (i + 1) % count) for i in range(count)])
    next_head = lax.ppermute(head, "region", [((i + 1) % count, i) for i in range(count)])
    windows = jnp.stack(
        [
            jnp.concatenate([prev_tail, emb[: 2 * block_size]], axis=0),
            jnp.concatenate([emb[seg_rows - 2 * block_size :], next_head], axis=0),
        ]
    )
    edge = smooth_edge(windows, nb_t, w_t, block_size)

    pred_rows, slot_grad = trip_pass(
        pair_block.reshape(-1),
        lengths,
        incoming,
        query_t,
        targets.reshape(trip_blocks, 1, block_size),
        trip_weight.reshape(trip_blocks, 1, block_size),
        inner,
    )
    predicted = pred_rows.reshape(trip_blocks * block_size)

    returned = lax.all_to_all(
        slot_grad.reshape(regions, slot_count, rank_width, block_size),
        "region",
        split_axis=0,
        concat_axis=0,
        tiled=True,
    )
    returned = returned.reshape(regions * slot_count, rank_width, block_size)

    target_rows = jnp.where(live_mask, send_rows, -1).reshape(-1)
    owned = owned_pass(target_rows, returned, edge, block_count).reshape(seg_rows, rank_width)
    partner = lax.ppermute(owned, "rep", [(0, 1), (1, 0)])
    smoothed = jnp.concatenate([edge[:block_size], inner, edge[block_size:]], axis=0)
    gradient = (owned + partner) + LAM * smoothed
    return (predicted, gradient.astype(jnp.bfloat16))


def solution(mesh):
    placed = (
        P("region", None),
        P(("region", "rep"), None, None, None),
        P(("region", "rep"), None),
        P(None, ("region", "rep")),
        P(),
        P(("region", "rep")),
        P(("region", "rep")),
        P("region", "rep", None, None),
        P("region", None, None),
        P("region", None, None),
    )
    return jax.shard_map(
        local,
        mesh=mesh,
        in_specs=placed,
        out_specs=(P(("region", "rep")), P("region", None)),
        check_vma=False,
    )
```

```python
import functools

import jax
import jax.numpy as jnp
from jax import lax
from jax.experimental import pallas as pl
from jax.experimental.pallas import tpu as pltpu
from jax.sharding import PartitionSpec as P

LAM = 0.25
F32 = jnp.float32
BF16 = jnp.bfloat16
TN = (((0,), (0,)), ((), ()))


def trip_kernel(
    pair_count, trip_steps, pb_ref, len_ref, inc_ref, qt_ref, tgt_ref, w_ref, _, pred_ref, out_ref,
    acc_ref,
):
    step = pl.program_id(0)
    per_step = len_ref.shape[0]
    block = qt_ref.shape[0]

    @pl.when(step == 0)
    def _():
        acc_ref[...] = jnp.zeros_like(acc_ref)

    @pl.when(step < trip_steps)
    def _():
        for u in range(per_step):
            t = step * per_step + u
            hidden = None
            for k in range(0, pair_count, 2):
                p0 = pb_ref[t * pair_count + k]
                p1 = pb_ref[t * pair_count + k + 1]
                lhs = jnp.concatenate([len_ref[u, k], len_ref[u, k + 1]], axis=1)
                rhs = jnp.concatenate([inc_ref[p0], inc_ref[p1]], axis=0)
                term = jnp.dot(lhs, rhs, preferred_element_type=F32)
                hidden = term if hidden is None else hidden + term
            q_t = qt_ref[:, u * block : (u + 1) * block]
            pred_row = jnp.sum(hidden.T * q_t, axis=0, keepdims=True)
            pred_ref[u] = pred_row
            err_row = w_ref[u] * (pred_row - tgt_ref[u])
            scaled_t = (err_row * q_t).astype(BF16)
            for k in range(pair_count):
                p = pb_ref[t * pair_count + k]
                acc_ref[p] += jnp.dot(scaled_t, len_ref[u, k], preferred_element_type=F32)

    @pl.when(step >= trip_steps)
    def _():
        chunk = out_ref.shape[0]
        first = pl.multiple_of((step - trip_steps) * chunk, chunk)
        out_ref[...] = acc_ref[pl.ds(first, chunk)].astype(out_ref.dtype)


def trip_pass(pair_flat, lengths, incoming, query_t, tgt, wts, after, per_step=12, flush=4):
    trip_blocks, pair_count, block, rank = lengths.shape
    slots = incoming.shape[0]
    trip_steps = trip_blocks // per_step
    chunk = slots // flush
    last = trip_steps - 1
    const3 = lambda t, pb: (0, 0, 0)
    return pl.pallas_call(
        functools.partial(trip_kernel, pair_count, trip_steps),
        grid_spec=pltpu.PrefetchScalarGridSpec(
            num_scalar_prefetch=1,
            grid=(trip_steps + flush,),
            in_specs=[
                pl.BlockSpec(
                    (per_step, pair_count, block, block),
                    lambda t, pb: (jnp.minimum(t, last), 0, 0, 0),
                ),
                pl.BlockSpec((slots, block, rank), const3, pipeline_mode=pl.Buffered(1)),
                pl.BlockSpec((rank, per_step * block), lambda t, pb: (0, jnp.minimum(t, last))),
                pl.BlockSpec((per_step, 1, block), lambda t, pb: (jnp.minimum(t, last), 0, 0)),
                pl.BlockSpec((per_step, 1, block), lambda t, pb: (jnp.minimum(t, last), 0, 0)),
                pl.BlockSpec(memory_space=pl.ANY),
            ],
            out_specs=[
                pl.BlockSpec((per_step, 1, block), lambda t, pb: (jnp.minimum(t, last), 0, 0)),
                pl.BlockSpec(
                    (chunk, block, rank), lambda t, pb: (jnp.maximum(t - trip_steps, 0), 0, 0)
                ),
            ],
            scratch_shapes=[pltpu.VMEM((slots, block, rank), F32)],
        ),
        out_shape=[
            jax.ShapeDtypeStruct((trip_blocks, 1, block), F32),
            jax.ShapeDtypeStruct((slots, block, rank), BF16),
        ],
        compiler_params=pltpu.CompilerParams(
            dimension_semantics=("arbitrary",), vmem_limit_bytes=60 * 1024 * 1024
        ),
    )(pair_flat, lengths, incoming, query_t, tgt, wts, after)


def band_of(nb_ref, w_ref, base, rows):
    span = 3 * rows
    row = lax.broadcasted_iota(jnp.int32, (span, rows), 0)
    band = jnp.zeros((span, rows), F32)
    for k in range(nb_ref.shape[0]):
        rel = nb_ref[k : k + 1, :] - base
        band = band - jnp.where(row == rel, w_ref[k : k + 1, :], 0.0)
    mid_row = lax.broadcasted_iota(jnp.int32, (rows, rows), 0)
    mid_col = lax.broadcasted_iota(jnp.int32, (rows, rows), 1)
    total = jnp.sum(w_ref[...], axis=0, keepdims=True)
    mid = band[rows : 2 * rows] + jnp.where(mid_row == mid_col, total, 0.0)
    band = jnp.concatenate([band[:rows], mid, band[2 * rows :]], axis=0)
    hi = band.astype(BF16)
    lo = (band - hi.astype(F32)).astype(BF16)
    return hi, lo


def apply_band(hi, lo, window):
    return lax.dot_general(hi, window, TN, preferred_element_type=F32) + lax.dot_general(
        lo, window, TN, preferred_element_type=F32
    )


def smooth_inner_kernel(emb_ref, nb_ref, w_ref, out_ref):
    rows = out_ref.shape[0]
    i = pl.program_id(0) + 1
    hi, lo = band_of(nb_ref, w_ref, i * rows, rows)
    window = emb_ref[pl.ds(pl.multiple_of((i - 1) * rows, rows), 3 * rows), :]
    out_ref[...] = apply_band(hi, lo, window)


def smooth_edge_kernel(last, win_ref, nb_ref, w_ref, out_ref):
    rows = out_ref.shape[0]
    i = pl.program_id(0) * last
    hi, lo = band_of(nb_ref, w_ref, i * rows, rows)
    out_ref[...] = apply_band(hi, lo, win_ref[0])


def smooth_inner(emb, nb_t, w_t, rows):
    seg_rows, rank = emb.shape
    inner = seg_rows // rows - 2
    return pl.pallas_call(
        smooth_inner_kernel,
        grid=(inner,),
        in_specs=[
            pl.BlockSpec(emb.shape, lambda i: (0, 0), pipeline_mode=pl.Buffered(1)),
            pl.BlockSpec((nb_t.shape[0], rows), lambda i: (0, i + 1)),
            pl.BlockSpec((w_t.shape[0], rows), lambda i: (0, i + 1)),
        ],
        out_specs=pl.BlockSpec((rows, rank), lambda i: (i, 0)),
        out_shape=jax.ShapeDtypeStruct((inner * rows, rank), F32),
        compiler_params=pltpu.CompilerParams(dimension_semantics=("arbitrary",)),
    )(emb, nb_t, w_t)


def smooth_edge(windows, nb_t, w_t, rows):
    rank = windows.shape[2]
    last = nb_t.shape[1] // rows - 1
    return pl.pallas_call(
        functools.partial(smooth_edge_kernel, last),
        grid=(2,),
        in_specs=[
            pl.BlockSpec((1,) + windows.shape[1:], lambda i: (i, 0, 0)),
            pl.BlockSpec((nb_t.shape[0], rows), lambda i: (0, i * last)),
            pl.BlockSpec((w_t.shape[0], rows), lambda i: (0, i * last)),
        ],
        out_specs=pl.BlockSpec((rows, rank), lambda i: (i, 0)),
        out_shape=jax.ShapeDtypeStruct((2 * rows, rank), F32),
        compiler_params=pltpu.CompilerParams(dimension_semantics=("arbitrary",)),
    )(windows, nb_t, w_t)


def owned_kernel(tgt_ref, ret_ref, _, out_ref):
    c = pl.program_id(0)
    chunk = ret_ref.shape[0]

    @pl.when(c == 0)
    def _():
        out_ref[...] = jnp.zeros_like(out_ref)

    for s in range(chunk):
        b = tgt_ref[c * chunk + s]

        @pl.when(b >= 0)
        def _():
            out_ref[b] += ret_ref[s].astype(F32)

    @pl.when(c == pl.num_programs(0) - 1)
    def _():
        for b in range(out_ref.shape[0]):
            out_ref[b] = out_ref[b].T


def owned_pass(targets, returned, after, block_count, chunk=128):
    slots, rank, block = returned.shape
    return pl.pallas_call(
        owned_kernel,
        grid_spec=pltpu.PrefetchScalarGridSpec(
            num_scalar_prefetch=1,
            grid=(slots // chunk,),
            in_specs=[
                pl.BlockSpec((chunk, rank, block), lambda c, tg: (c, 0, 0)),
                pl.BlockSpec(memory_space=pl.ANY),
            ],
            out_specs=pl.BlockSpec(
                (block_count, rank, block), lambda c, tg: (0, 0, 0), pipeline_mode=pl.Buffered(1)
            ),
        ),
        out_shape=jax.ShapeDtypeStruct((block_count, rank, block), F32),
        compiler_params=pltpu.CompilerParams(dimension_semantics=("arbitrary",)),
    )(targets, returned, after)


def gather_kernel(idx_ref, src_ref, out_ref):
    c = pl.program_id(0)
    chunk = out_ref.shape[0]
    for s in range(chunk):
        out_ref[s] = src_ref[idx_ref[c * chunk + s]]


def gather_blocks(idx, blocks, chunk=128):
    count = idx.shape[0]
    return pl.pallas_call(
        gather_kernel,
        grid_spec=pltpu.PrefetchScalarGridSpec(
            num_scalar_prefetch=1,
            grid=(count // chunk,),
            in_specs=[
                pl.BlockSpec(blocks.shape, lambda c, ix: (0, 0, 0), pipeline_mode=pl.Buffered(1))
            ],
            out_specs=pl.BlockSpec((chunk,) + blocks.shape[1:], lambda c, ix: (c, 0, 0)),
        ),
        out_shape=jax.ShapeDtypeStruct((count,) + blocks.shape[1:], blocks.dtype),
    )(idx, blocks)


def local(
    emb, lengths, pair_block, feats, proj, targets, trip_weight, send_list, nb_index, nb_weight
):
    block_size = lengths.shape[2]
    rank_width = emb.shape[1]
    seg_rows = emb.shape[0]
    block_count = seg_rows // block_size
    regions = lax.axis_size("region")
    blocks = emb.reshape(block_count, block_size, rank_width)
    send_rows = send_list[0, 0]
    live_mask = send_rows >= 0
    slot_count = send_rows.shape[1]
    outgoing = gather_blocks(jnp.where(live_mask, send_rows, 0).reshape(-1), blocks)
    outgoing = outgoing.reshape(regions, slot_count, block_size, rank_width)
    incoming = lax.all_to_all(outgoing, "region", split_axis=0, concat_axis=0, tiled=True)
    incoming = incoming.reshape(regions * slot_count, block_size, rank_width)
    trip_blocks = lengths.shape[0]
    query_t = jnp.einsum("fr,ft->rt", proj, feats, preferred_element_type=F32)

    nb_t = nb_index[0]
    w_t = nb_weight[0]
    inner = smooth_inner(emb, nb_t, w_t, block_size)
    count = regions
    head = emb[:block_size]
    tail = emb[seg_rows - block_size :]
    prev_tail = lax.ppermute(tail, "region", [(i, (i + 1) % count) for i in range(count)])
    next_head = lax.ppermute(head, "region", [((i + 1) % count, i) for i in range(count)])
    windows = jnp.stack(
        [
            jnp.concatenate([prev_tail, emb[: 2 * block_size]], axis=0),
            jnp.concatenate([emb[seg_rows - 2 * block_size :], next_head], axis=0),
        ]
    )
    edge = smooth_edge(windows, nb_t, w_t, block_size)

    pred_rows, slot_grad = trip_pass(
        pair_block.reshape(-1),
        lengths,
        incoming,
        query_t,
        targets.reshape(trip_blocks, 1, block_size),
        trip_weight.reshape(trip_blocks, 1, block_size),
        inner,
    )
    predicted = pred_rows.reshape(trip_blocks * block_size)

    returned = lax.all_to_all(
        slot_grad.reshape(regions, slot_count, rank_width, block_size),
        "region",
        split_axis=0,
        concat_axis=0,
        tiled=True,
    )
    returned = returned.reshape(regions * slot_count, rank_width, block_size)

    target_rows = jnp.where(live_mask, send_rows, -1).reshape(-1)
    owned = owned_pass(target_rows, returned, edge, block_count).reshape(seg_rows, rank_width)
    partner = lax.ppermute(owned, "rep", [(0, 1), (1, 0)])
    smoothed = jnp.concatenate([edge[:block_size], inner, edge[block_size:]], axis=0)
    gradient = (owned + partner) + LAM * smoothed
    return (predicted, gradient.astype(jnp.bfloat16))


def solution(mesh):
    placed = (
        P("region", None),
        P(("region", "rep"), None, None, None),
        P(("region", "rep"), None),
        P(None, ("region", "rep")),
        P(),
        P(("region", "rep")),
        P(("region", "rep")),
        P("region", "rep", None, None),
        P("region", None, None),
        P("region", None, None),
    )
    return jax.shard_map(
        local,
        mesh=mesh,
        in_specs=placed,
        out_specs=(P(("region", "rep")), P("region", None)),
        check_vma=False,
    )
```

```python
import functools

import jax
import jax.numpy as jnp
from jax import lax
from jax.experimental import pallas as pl
from jax.experimental.pallas import tpu as pltpu
from jax.sharding import PartitionSpec as P

LAM = 0.25
F32 = jnp.float32
BF16 = jnp.bfloat16
TN = (((0,), (0,)), ((), ()))


def trip_kernel(
    pair_count, trip_steps, pb_ref, len_ref, inc_ref, qt_ref, tgt_ref, w_ref, _, pred_ref, out_ref,
    acc_ref,
):
    step = pl.program_id(0)
    per_step = len_ref.shape[0]
    block = qt_ref.shape[0]

    @pl.when(step == 0)
    def _():
        acc_ref[...] = jnp.zeros_like(acc_ref)

    @pl.when(step < trip_steps)
    def _():
        for u in range(per_step):
            t = step * per_step + u
            hidden = None
            for k in range(0, pair_count, 2):
                p0 = pb_ref[t * pair_count + k]
                p1 = pb_ref[t * pair_count + k + 1]
                lhs = jnp.concatenate([len_ref[u, k], len_ref[u, k + 1]], axis=1)
                rhs = jnp.concatenate([inc_ref[p0], inc_ref[p1]], axis=0)
                term = jnp.dot(lhs, rhs, preferred_element_type=F32)
                hidden = term if hidden is None else hidden + term
            q_t = qt_ref[:, u * block : (u + 1) * block]
            pred_row = jnp.sum(hidden.T * q_t, axis=0, keepdims=True)
            pred_ref[u] = pred_row
            err_row = w_ref[u] * (pred_row - tgt_ref[u])
            scaled_t = (err_row * q_t).astype(BF16)
            for k in range(0, pair_count, 2):
                p0 = pb_ref[t * pair_count + k]
                p1 = pb_ref[t * pair_count + k + 1]
                rhs = jnp.concatenate([len_ref[u, k], len_ref[u, k + 1]], axis=1)
                both = jnp.dot(scaled_t, rhs, preferred_element_type=F32)
                acc_ref[p0] += both[:, :block]
                acc_ref[p1] += both[:, block:]

    @pl.when(step >= trip_steps)
    def _():
        chunk = out_ref.shape[0]
        first = pl.multiple_of((step - trip_steps) * chunk, chunk)
        out_ref[...] = acc_ref[pl.ds(first, chunk)].astype(out_ref.dtype)


def trip_pass(pair_flat, lengths, incoming, query_t, tgt, wts, after, per_step=12, flush=4):
    trip_blocks, pair_count, block, rank = lengths.shape
    slots = incoming.shape[0]
    trip_steps = trip_blocks // per_step
    chunk = slots // flush
    last = trip_steps - 1
    const3 = lambda t, pb: (0, 0, 0)
    return pl.pallas_call(
        functools.partial(trip_kernel, pair_count, trip_steps),
        grid_spec=pltpu.PrefetchScalarGridSpec(
            num_scalar_prefetch=1,
            grid=(trip_steps + flush,),
            in_specs=[
                pl.BlockSpec(
                    (per_step, pair_count, block, block),
                    lambda t, pb: (jnp.minimum(t, last), 0, 0, 0),
                ),
                pl.BlockSpec((slots, block, rank), const3, pipeline_mode=pl.Buffered(1)),
                pl.BlockSpec((rank, per_step * block), lambda t, pb: (0, jnp.minimum(t, last))),
                pl.BlockSpec((per_step, 1, block), lambda t, pb: (jnp.minimum(t, last), 0, 0)),
                pl.BlockSpec((per_step, 1, block), lambda t, pb: (jnp.minimum(t, last), 0, 0)),
                pl.BlockSpec(memory_space=pl.ANY),
            ],
            out_specs=[
                pl.BlockSpec((per_step, 1, block), lambda t, pb: (jnp.minimum(t, last), 0, 0)),
                pl.BlockSpec(
                    (chunk, block, rank), lambda t, pb: (jnp.maximum(t - trip_steps, 0), 0, 0)
                ),
            ],
            scratch_shapes=[pltpu.VMEM((slots, block, rank), F32)],
        ),
        out_shape=[
            jax.ShapeDtypeStruct((trip_blocks, 1, block), F32),
            jax.ShapeDtypeStruct((slots, block, rank), BF16),
        ],
        compiler_params=pltpu.CompilerParams(
            dimension_semantics=("arbitrary",), vmem_limit_bytes=60 * 1024 * 1024
        ),
    )(pair_flat, lengths, incoming, query_t, tgt, wts, after)


def band_of(nb_ref, w_ref, base, rows):
    span = 3 * rows
    row = lax.broadcasted_iota(jnp.int32, (span, rows), 0)
    band = jnp.zeros((span, rows), F32)
    for k in range(nb_ref.shape[0]):
        rel = nb_ref[k : k + 1, :] - base
        band = band - jnp.where(row == rel, w_ref[k : k + 1, :], 0.0)
    mid_row = lax.broadcasted_iota(jnp.int32, (rows, rows), 0)
    mid_col = lax.broadcasted_iota(jnp.int32, (rows, rows), 1)
    total = jnp.sum(w_ref[...], axis=0, keepdims=True)
    mid = band[rows : 2 * rows] + jnp.where(mid_row == mid_col, total, 0.0)
    band = jnp.concatenate([band[:rows], mid, band[2 * rows :]], axis=0)
    hi = band.astype(BF16)
    lo = (band - hi.astype(F32)).astype(BF16)
    return hi, lo


def apply_band(hi, lo, window):
    return lax.dot_general(hi, window, TN, preferred_element_type=F32) + lax.dot_general(
        lo, window, TN, preferred_element_type=F32
    )


def smooth_inner_kernel(emb_ref, nb_ref, w_ref, out_ref):
    rows = out_ref.shape[0]
    i = pl.program_id(0) + 1
    hi, lo = band_of(nb_ref, w_ref, i * rows, rows)
    window = emb_ref[pl.ds(pl.multiple_of((i - 1) * rows, rows), 3 * rows), :]
    out_ref[...] = apply_band(hi, lo, window)


def smooth_edge_kernel(last, win_ref, nb_ref, w_ref, out_ref):
    rows = out_ref.shape[0]
    i = pl.program_id(0) * last
    hi, lo = band_of(nb_ref, w_ref, i * rows, rows)
    out_ref[...] = apply_band(hi, lo, win_ref[0])


def smooth_inner(emb, nb_t, w_t, rows):
    seg_rows, rank = emb.shape
    inner = seg_rows // rows - 2
    return pl.pallas_call(
        smooth_inner_kernel,
        grid=(inner,),
        in_specs=[
            pl.BlockSpec(emb.shape, lambda i: (0, 0), pipeline_mode=pl.Buffered(1)),
            pl.BlockSpec((nb_t.shape[0], rows), lambda i: (0, i + 1)),
            pl.BlockSpec((w_t.shape[0], rows), lambda i: (0, i + 1)),
        ],
        out_specs=pl.BlockSpec((rows, rank), lambda i: (i, 0)),
        out_shape=jax.ShapeDtypeStruct((inner * rows, rank), F32),
        compiler_params=pltpu.CompilerParams(dimension_semantics=("arbitrary",)),
    )(emb, nb_t, w_t)


def smooth_edge(windows, nb_t, w_t, rows):
    rank = windows.shape[2]
    last = nb_t.shape[1] // rows - 1
    return pl.pallas_call(
        functools.partial(smooth_edge_kernel, last),
        grid=(2,),
        in_specs=[
            pl.BlockSpec((1,) + windows.shape[1:], lambda i: (i, 0, 0)),
            pl.BlockSpec((nb_t.shape[0], rows), lambda i: (0, i * last)),
            pl.BlockSpec((w_t.shape[0], rows), lambda i: (0, i * last)),
        ],
        out_specs=pl.BlockSpec((rows, rank), lambda i: (i, 0)),
        out_shape=jax.ShapeDtypeStruct((2 * rows, rank), F32),
        compiler_params=pltpu.CompilerParams(dimension_semantics=("arbitrary",)),
    )(windows, nb_t, w_t)


def owned_kernel(tgt_ref, ret_ref, _, out_ref):
    c = pl.program_id(0)
    chunk = ret_ref.shape[0]

    @pl.when(c == 0)
    def _():
        out_ref[...] = jnp.zeros_like(out_ref)

    for s in range(chunk):
        b = tgt_ref[c * chunk + s]

        @pl.when(b >= 0)
        def _():
            out_ref[b] += ret_ref[s].astype(F32)

    @pl.when(c == pl.num_programs(0) - 1)
    def _():
        for b in range(out_ref.shape[0]):
            out_ref[b] = out_ref[b].T


def owned_pass(targets, returned, after, block_count, chunk=128):
    slots, rank, block = returned.shape
    return pl.pallas_call(
        owned_kernel,
        grid_spec=pltpu.PrefetchScalarGridSpec(
            num_scalar_prefetch=1,
            grid=(slots // chunk,),
            in_specs=[
                pl.BlockSpec((chunk, rank, block), lambda c, tg: (c, 0, 0)),
                pl.BlockSpec(memory_space=pl.ANY),
            ],
            out_specs=pl.BlockSpec(
                (block_count, rank, block), lambda c, tg: (0, 0, 0), pipeline_mode=pl.Buffered(1)
            ),
        ),
        out_shape=jax.ShapeDtypeStruct((block_count, rank, block), F32),
        compiler_params=pltpu.CompilerParams(dimension_semantics=("arbitrary",)),
    )(targets, returned, after)


def gather_kernel(idx_ref, src_ref, out_ref):
    c = pl.program_id(0)
    chunk = out_ref.shape[0]
    for s in range(chunk):
        out_ref[s] = src_ref[idx_ref[c * chunk + s]]


def gather_blocks(idx, blocks, chunk=64):
    count = idx.shape[0]
    return pl.pallas_call(
        gather_kernel,
        grid_spec=pltpu.PrefetchScalarGridSpec(
            num_scalar_prefetch=1,
            grid=(count // chunk,),
            in_specs=[
                pl.BlockSpec(blocks.shape, lambda c, ix: (0, 0, 0), pipeline_mode=pl.Buffered(1))
            ],
            out_specs=pl.BlockSpec((chunk,) + blocks.shape[1:], lambda c, ix: (c, 0, 0)),
        ),
        out_shape=jax.ShapeDtypeStruct((count,) + blocks.shape[1:], blocks.dtype),
    )(idx, blocks)


def local(
    emb, lengths, pair_block, feats, proj, targets, trip_weight, send_list, nb_index, nb_weight
):
    block_size = lengths.shape[2]
    rank_width = emb.shape[1]
    seg_rows = emb.shape[0]
    block_count = seg_rows // block_size
    regions = lax.axis_size("region")
    blocks = emb.reshape(block_count, block_size, rank_width)
    send_rows = send_list[0, 0]
    live_mask = send_rows >= 0
    slot_count = send_rows.shape[1]
    outgoing = gather_blocks(jnp.where(live_mask, send_rows, 0).reshape(-1), blocks)
    outgoing = outgoing.reshape(regions, slot_count, block_size, rank_width)
    incoming = lax.all_to_all(outgoing, "region", split_axis=0, concat_axis=0, tiled=True)
    incoming = incoming.reshape(regions * slot_count, block_size, rank_width)
    trip_blocks = lengths.shape[0]
    query_t = jnp.einsum("fr,ft->rt", proj, feats, preferred_element_type=F32)

    nb_t = nb_index[0]
    w_t = nb_weight[0]
    inner = smooth_inner(emb, nb_t, w_t, block_size)
    count = regions
    head = emb[:block_size]
    tail = emb[seg_rows - block_size :]
    prev_tail = lax.ppermute(tail, "region", [(i, (i + 1) % count) for i in range(count)])
    next_head = lax.ppermute(head, "region", [((i + 1) % count, i) for i in range(count)])
    windows = jnp.stack(
        [
            jnp.concatenate([prev_tail, emb[: 2 * block_size]], axis=0),
            jnp.concatenate([emb[seg_rows - 2 * block_size :], next_head], axis=0),
        ]
    )
    edge = smooth_edge(windows, nb_t, w_t, block_size)

    pred_rows, slot_grad = trip_pass(
        pair_block.reshape(-1),
        lengths,
        incoming,
        query_t,
        targets.reshape(trip_blocks, 1, block_size),
        trip_weight.reshape(trip_blocks, 1, block_size),
        inner,
    )
    predicted = pred_rows.reshape(trip_blocks * block_size)

    returned = lax.all_to_all(
        slot_grad.reshape(regions, slot_count, rank_width, block_size),
        "region",
        split_axis=0,
        concat_axis=0,
        tiled=True,
    )
    returned = returned.reshape(regions * slot_count, rank_width, block_size)

    target_rows = jnp.where(live_mask, send_rows, -1).reshape(-1)
    owned = owned_pass(target_rows, returned, edge, block_count).reshape(seg_rows, rank_width)
    partner = lax.ppermute(owned, "rep", [(0, 1), (1, 0)])
    smoothed = jnp.concatenate([edge[:block_size], inner, edge[block_size:]], axis=0)
    gradient = (owned + partner) + LAM * smoothed
    return (predicted, gradient.astype(jnp.bfloat16))


def solution(mesh):
    placed = (
        P("region", None),
        P(("region", "rep"), None, None, None),
        P(("region", "rep"), None),
        P(None, ("region", "rep")),
        P(),
        P(("region", "rep")),
        P(("region", "rep")),
        P("region", "rep", None, None),
        P("region", None, None),
        P("region", None, None),
    )
    return jax.shard_map(
        local,
        mesh=mesh,
        in_specs=placed,
        out_specs=(P(("region", "rep")), P("region", None)),
        check_vma=False,
    )
```
